128 devices in a mesh: row: 8 (over z, core), col: 16 (over x, y).
Axes of the slice: x: 4, y: 4, z: 4, core: 2. Of those that a mesh axis runs over, the one named last changes fastest.
Arguments:
- tokens: bfloat16 [4096, 2048], P('col', 'row'), may hold values from -6 to 6
- router: bfloat16 [2048, 32], replicated, may hold values from -0.125 to 0.125
- shared_gate_vector: bfloat16 [2048], replicated, may hold values from -0.125 to 0.125
- shared_gate_weight: bfloat16 [2048, 5632], P('col', 'row'), may hold values from -0.125 to 0.125
- shared_up_weight: bfloat16 [2048, 5632], P('col', 'row'), may hold values from -0.125 to 0.125
- shared_down_weight: bfloat16 [5632, 2048], P('row', 'col'), may hold values from -0.078125 to 0.078125
- routed_gate_weight: bfloat16 [32, 2048, 1408], P('col', None, 'row'), may hold values from -0.125 to 0.125
- routed_up_weight: bfloat16 [32, 2048, 1408], P('col', None, 'row'), may hold values from -0.125 to 0.125
- routed_down_weight: bfloat16 [32, 1408, 2048], P('col', 'row'), may hold values from -0.15625 to 0.15625
- adapter_input_factor: bfloat16 [64, 16, 2048], P(None, None, 'row'), may hold values from -0.125 to 0.125
- adapter_output_factor: bfloat16 [64, 16, 5632], P(None, None, 'row'), may hold values from -0.29882812 to 0.29882812
- routes: int32 [4096, 4], P('col'), may hold values from 0 to 31, all different within a row; in each aligned block of 256 rows (0 to 255, 256 to 511, ...) at most 64 rows name the same one
- lengths: int32 [16, 16], P('col'), may hold values from 1 to 128, 256 in all within a row
- prompt_adapter_index: int32 [16, 16], P('col'), may hold values from 0 to 15
- active_adapter_index: int32 [16], replicated, may hold values from 0 to 63, as said below
Outputs:
- moe_out: float32 [4096, 2048], P('col', 'row')
The draws below stay inside these ranges and needn't reach their ends.
Inputs may be any that keep to these rules, and one draw needn't show every extreme that they name: `routes`: in each group of 256 consecutive tokens no expert is named by more than 64 tokens, a bound that some block reaches. Each group's 16 lengths sum to 256; the longest is exactly 128. `active_adapter_index`: the 16 entries are distinct.
All inputs are finite; a program needn't handle non-finite values.
Results may differ from the reference program's by a relative error of at most 0.003.
Values may be sent and summed in bfloat16 or wider, within the bound.
No kernel may reach another device: no remote copies, remote signals or barrier semaphores. Data moves between devices by JAX's collectives and lax.ppermute only.
A program may use at most 128 MiB of HBM per device.

```python
import math
import jax
import jax.numpy as jnp
import numpy as np
from jax import lax

MODEL_WIDTH = 2048
FF = 1408
SHARED_UNITS = 5632
TOP = 4
ADAPTER_RANK = 16
ADAPTER_COUNT = 64
NACT = 16
TOK_DEV = 256
NREQ = 16
PROMPT_MAX = 128
GROUPS = 16
TOKENS = 4096
EXPERTS = 32
CAP = 64
N_COL = 16


def draw_active_adapter_index(key, part):
    order = jax.random.permutation(key, ADAPTER_COUNT)
    return order[:NACT].astype(jnp.int32)


def plant(drawn, own_key, low, top_value):
    longest = drawn.shape.index(max(drawn.shape))
    spots = []
    for shift in (0, 1):
        where = [jax.random.randint(jax.random.fold_in(own_key, axis), (), 0, length) for axis, length in enumerate(drawn.shape)]
        where[longest] = (where[longest] + shift) % drawn.shape[longest]
        spots.append(tuple(where))
    return drawn.at[spots[0]].set(low).at[spots[1]].set(top_value)


def block_levels(rng, dims, cuts, low, top_value):
    factor_of = 1.0
    for dim, shards_of in cuts:
        heights = jax.random.uniform(jax.random.fold_in(jax.random.fold_in(rng, 6), dim), (shards_of,), jnp.float32, low / len(cuts), top_value / len(cuts))
        factor_of = factor_of * jnp.repeat(jnp.exp(heights), dims[dim] // shards_of).reshape((-1,) + (1,) * (len(dims) - 1 - dim))
    return factor_of


def length_profile(amount, total, most, lean):
    weights = [(1 << 20) // math.isqrt(standing ** lean) + 1 for standing in range(2, amount + 1)]
    spare, counts = total - most - (amount - 1), [1] * (amount - 1)
    while spare > 0:
        free = [i for i in range(amount - 1) if counts[i] < most]
        whole, remaining = sum([weights[i] for i in free]), spare
        for i in free:
            more = min(most - counts[i], max(1, remaining * weights[i] // whole), spare)
            counts[i] = counts[i] + more
            spare = spare - more
    return np.array([most] + counts)


def ragged(own_key, number_of, total, reach, slope):
    if number_of == 2:
        one = jax.random.randint(own_key, (), max(1, total - reach), min(reach, total - 1) + 1)
        return jnp.stack([one, total - one])
    sizes = jnp.asarray(length_profile(number_of, total, reach, slope), jnp.int32)
    couples = (number_of - 1) // 2
    giver, taker = sizes[1:1 + 2 * couples:2], sizes[2:2 + 2 * couples:2]
    margin = jnp.minimum(giver - 1, reach - taker)
    shifted = jax.random.randint(jax.random.fold_in(own_key, 1), (couples,), 0, 1 << 20) % (margin + 1)
    sizes = sizes.at[1:1 + 2 * couples:2].set(giver - shifted).at[2:2 + 2 * couples:2].set(taker + shifted)
    return sizes[jax.random.permutation(jax.random.fold_in(own_key, 2), number_of)]


def deal_out(own_key, own, number, rows, count, top, limit, lean):
    ranking = jax.random.permutation(own_key, count)
    crowded, common = shares(count, rows * top, limit, lean, True), shares(count, rows * top, limit, lean, False)
    places = jnp.arange(count)

    def named(tallies, turn):
        used = int((tallies > 0).sum())
        fixed = max(1, used // 4)
        passed = fixed + (places - fixed + turn * (used - fixed)) % max(1, count - fixed)
        return jnp.zeros((count,), jnp.int32).at[ranking[jnp.where(places < fixed, places, passed)]].set(jnp.asarray(tallies, jnp.int32))

    tallies = jnp.where(number % 4 == 0, named(crowded, number // 4), named(common, number - number // 4 - 1))
    mixed = jax.random.permutation(jax.random.fold_in(own, 3), count)
    donor, receiver = mixed[0:count // 2 * 2:2], mixed[1:count // 2 * 2:2]
    margin = jnp.minimum(tallies[donor] - 1, limit - tallies[receiver]) // 2
    margin = jnp.where((donor == ranking[0]) | (receiver == ranking[0]) | (tallies[receiver] == 0), 0, jnp.maximum(margin, 0))
    passed = jax.random.randint(jax.random.fold_in(own, 4), (count // 2,), 0, 1 << 20) % (margin + 1)
    tallies = tallies.at[donor].add(-passed).at[receiver].add(passed)
    items = jnp.searchsorted(jnp.cumsum(tallies), jnp.arange(rows * top), side="right").astype(jnp.int32)
    grid = items.reshape(top, rows).T
    grid = grid[jax.random.permutation(jax.random.fold_in(own, 1), rows)]
    turn = jax.random.randint(jax.random.fold_in(own, 2), (rows, 1), 0, top)
    return jnp.take_along_axis(grid, (jnp.arange(top)[None, :] + turn) % top, axis=1)


def shares(amount, total, most, slope, full):
    weights = [(1 << 20) // math.isqrt(grade ** slope) + 1 for grade in range(1, amount + 1)]
    largest = most if full else min(most, max(-(-total // amount), total * weights[0] // sum(weights)))
    least = 1 if total - largest >= amount - 1 else 0
    holding, surplus = [largest] + [least] * (amount - 1), total - largest - least * (amount - 1)
    while surplus > 0:
        movable = [i for i in range(1, amount) if holding[i] < largest] or [i for i in range(1, amount) if holding[i] < most]
        whole, remaining = sum([weights[i] for i in movable]), surplus
        for i in movable:
            addition = min(most - holding[i], max(1, remaining * weights[i] // whole), surplus)
            holding[i] = holding[i] + addition
            surplus = surplus - addition
    return np.array(holding)


def scatter_about(key, extent, spread, bound, shards=(), kind=jnp.bfloat16):
    result = spread * jax.random.normal(key, extent, jnp.float32)
    if shards:
        result = result * block_levels(key, extent, shards, -0.22, 0.18)
    return jnp.clip(result, -bound, bound).astype(kind)


def setup_inputs(seed: int = 0) -> dict:
    arg_keys = jax.random.split(jax.random.key(seed), 16)
    tokens = scatter_about(arg_keys[0], (TOKENS, MODEL_WIDTH), 1.0, 6.0, ((0, 16), (1, 8)))
    router = scatter_about(arg_keys[1], (MODEL_WIDTH, EXPERTS), MODEL_WIDTH ** -0.5, 0.125)
    shared_gate_vector = scatter_about(arg_keys[2], (MODEL_WIDTH,), MODEL_WIDTH ** -0.5, 0.125)
    shared_gate_weight = scatter_about(arg_keys[3], (MODEL_WIDTH, SHARED_UNITS), MODEL_WIDTH ** -0.5, 0.125, ((0, 16), (1, 8)))
    shared_up_weight = scatter_about(arg_keys[4], (MODEL_WIDTH, SHARED_UNITS), MODEL_WIDTH ** -0.5, 0.125, ((0, 16), (1, 8)))
    shared_down_weight = scatter_about(arg_keys[5], (SHARED_UNITS, MODEL_WIDTH), SHARED_UNITS ** -0.5, 0.078125, ((0, 8), (1, 16)))
    routed_gate_weight = scatter_about(arg_keys[6], (EXPERTS, MODEL_WIDTH, FF), MODEL_WIDTH ** -0.5, 0.125, ((0, 16), (2, 8)))
    routed_up_weight = scatter_about(arg_keys[7], (EXPERTS, MODEL_WIDTH, FF), MODEL_WIDTH ** -0.5, 0.125, ((0, 16), (2, 8)))
    routed_down_weight = scatter_about(arg_keys[8], (EXPERTS, FF, MODEL_WIDTH), FF ** -0.5, 0.15625, ((0, 16), (1, 8)))
    adapter_input_factor = scatter_about(arg_keys[9], (ADAPTER_COUNT, ADAPTER_RANK, MODEL_WIDTH), MODEL_WIDTH ** -0.5, 0.125, ((2, 8),))
    adapter_output_factor = scatter_about(arg_keys[10], (ADAPTER_COUNT, ADAPTER_RANK, SHARED_UNITS), 0.05, 0.29882812, ((2, 8),))
    routes_keys = jax.random.split(jax.random.fold_in(arg_keys[11], 1), TOKENS // TOK_DEV)
    routes_turns = jax.random.permutation(jax.random.fold_in(arg_keys[11], 3), TOKENS // TOK_DEV)
    routes = jax.vmap(lambda own, number: deal_out(jax.random.fold_in(arg_keys[11], 2), own, number, TOK_DEV, EXPERTS, TOP, CAP, 2))(routes_keys, routes_turns).reshape((TOKENS, TOP))
    lengths = jax.vmap(lambda own: ragged(own, NREQ, TOK_DEV, PROMPT_MAX, 2))(jax.random.split(arg_keys[12], GROUPS)).reshape((GROUPS, NREQ)).astype(jnp.int32)
    prompt_adapter_index = plant(jax.random.randint(arg_keys[13], (GROUPS, NREQ), 0, NACT), jax.random.fold_in(arg_keys[13], 1), 0, NACT - 1).astype(jnp.int32)
    active_adapter_index = draw_active_adapter_index(jax.random.fold_in(arg_keys[15], 71), 0)
    return {"tokens": tokens, "router": router, "shared_gate_vector": shared_gate_vector, "shared_gate_weight": shared_gate_weight, "shared_up_weight": shared_up_weight, "shared_down_weight": shared_down_weight, "routed_gate_weight": routed_gate_weight, "routed_up_weight": routed_up_weight, "routed_down_weight": routed_down_weight, "adapter_input_factor": adapter_input_factor, "adapter_output_factor": adapter_output_factor, "routes": routes, "lengths": lengths, "prompt_adapter_index": prompt_adapter_index, "active_adapter_index": active_adapter_index}


ADAPTER_SCALE = 2.0


def reference(tokens, router, shared_gate_vector, shared_gate_weight, shared_up_weight, shared_down_weight, routed_gate_weight, routed_up_weight, routed_down_weight, adapter_input_factor, adapter_output_factor, routes, lengths, prompt_adapter_index, active_adapter_index):
    logits = jnp.dot(tokens, router, preferred_element_type=jnp.float32)
    picked = jnp.take_along_axis(logits, routes, axis=1)
    raw_exp = jnp.exp(picked)
    gate_weights = raw_exp / jnp.sum(raw_exp, axis=1, keepdims=True)
    share = jax.nn.sigmoid(jnp.dot(tokens, shared_gate_vector, preferred_element_type=jnp.float32))

    request_ends = jnp.cumsum(lengths, axis=1).astype(jnp.int32)
    position = jnp.arange(TOK_DEV, dtype=jnp.int32)
    request_of = jnp.sum((position[None, :, None] >= request_ends[:, None, :]).astype(jnp.int32), axis=2).astype(jnp.int32)
    slot_of = jnp.take_along_axis(prompt_adapter_index, request_of, axis=1).reshape(TOKENS)
    reduced_rank_value = NACT * ADAPTER_RANK
    picked_input_factor = jnp.take(adapter_input_factor, active_adapter_index, axis=0).reshape(reduced_rank_value, MODEL_WIDTH)
    picked_output_factor = jnp.take(adapter_output_factor, active_adapter_index, axis=0).reshape(reduced_rank_value, SHARED_UNITS)
    low_rank = lax.dot_general(tokens, picked_input_factor, (((1,), (1,)), ((), ())), preferred_element_type=jnp.float32).astype(jnp.bfloat16)
    owner = (jnp.arange(reduced_rank_value, dtype=jnp.int32) // ADAPTER_RANK).astype(jnp.int32)
    adapter_mask = slot_of[:, None] == owner[None, :]
    low_masked = jnp.where(adapter_mask, low_rank, jnp.zeros((), jnp.bfloat16))
    adapter_update = jnp.dot(low_masked, picked_output_factor, preferred_element_type=jnp.float32)
    shared_gate_value = jnp.dot(tokens, shared_gate_weight, preferred_element_type=jnp.float32)
    shared_up_value = jnp.dot(tokens, shared_up_weight, preferred_element_type=jnp.float32) + ADAPTER_SCALE * adapter_update
    shared_hidden_units = (jax.nn.silu(shared_gate_value) * shared_up_value).astype(jnp.bfloat16)
    shared_out = jnp.dot(shared_hidden_units, shared_down_weight, preferred_element_type=jnp.float32)

    slots_all = N_COL * CAP
    slot_index = jnp.arange(slots_all, dtype=jnp.int32)

    def run_expert(packed):
        weights_gate, weights_up, weights_down, expert_id = packed
        hit_flags = jnp.any(routes == expert_id, axis=1).astype(jnp.int32)
        running = jnp.cumsum(hit_flags).astype(jnp.int32)
        slot_token = jnp.sum((running[None, :] <= slot_index[:, None]).astype(jnp.int32), axis=1).astype(jnp.int32)
        slot_valid = slot_index < running[-1]
        gathered = jnp.take(tokens, jnp.minimum(slot_token, TOKENS - 1), axis=0)
        gathered = jnp.where(slot_valid[:, None], gathered, jnp.zeros((), jnp.bfloat16))
        gate_part = jnp.dot(gathered, weights_gate, preferred_element_type=jnp.float32)
        up_part = jnp.dot(gathered, weights_up, preferred_element_type=jnp.float32)
        hidden = (jax.nn.silu(gate_part) * up_part).astype(jnp.bfloat16)
        return jnp.dot(hidden, weights_down, preferred_element_type=jnp.float32)

    expert_rows = lax.map(run_expert, (routed_gate_weight, routed_up_weight, routed_down_weight, jnp.arange(EXPERTS, dtype=jnp.int32)))
    onehot = routes[:, :, None] == jnp.arange(EXPERTS, dtype=jnp.int32)[None, None, :]
    hit_table = jnp.any(onehot, axis=1).astype(jnp.int32)
    slot_rank = (jnp.cumsum(hit_table, axis=0) - hit_table).astype(jnp.int32)
    route_rank = jnp.sum(jnp.where(onehot, slot_rank[:, None, :], 0), axis=2).astype(jnp.int32)
    row_index = (routes * slots_all + route_rank).astype(jnp.int32)
    routed_rows = jnp.take(expert_rows.reshape(EXPERTS * slots_all, MODEL_WIDTH), row_index, axis=0)
    routed = jnp.sum(gate_weights[:, :, None] * routed_rows, axis=1)
    return routed + share[:, None] * shared_out
```

```python
import jax
import jax.numpy as jnp
from jax import lax
from jax.sharding import PartitionSpec as P

ADAPTER_SCALE = 2.0


def on_device(
    tokens,
    router,
    shared_gate_vector,
    shared_gate_weight,
    shared_up_weight,
    shared_down_weight,
    routed_gate_weight,
    routed_up_weight,
    routed_down_weight,
    adapter_input_factor,
    adapter_output_factor,
    routes,
    lengths,
    prompt_adapter_index,
    active_adapter_index,
):
    row_count = lax.axis_size("row")
    col_count = lax.axis_size("col")
    row_id = lax.axis_index("row")
    token_count = tokens.shape[0]
    local_width = tokens.shape[1]
    picked_input_factor = jnp.take(adapter_input_factor, active_adapter_index, axis=0)
    rank_width = picked_input_factor.shape[1]
    reduced_rank_value = picked_input_factor.shape[0] * rank_width
    gathered = lax.all_gather(
        jnp.concatenate(
            [tokens, picked_input_factor.reshape(reduced_rank_value, local_width)], axis=0
        ),
        "row",
        axis=1,
        tiled=True,
    )
    all_features = gathered[:token_count]
    full_in = gathered[token_count:]
    full_width = all_features.shape[1]
    local_experts = routed_gate_weight.shape[0]
    expert_count = local_experts * col_count
    route_count = routes.shape[1]
    capacity = 2 * token_count * route_count // expert_count

    shared_stack = jnp.stack(
        [shared_gate_weight, shared_up_weight, shared_down_weight.T], axis=0
    )
    shared_full = lax.all_gather(shared_stack, "col", axis=1, tiled=True)

    down_by_feature = lax.all_to_all(
        routed_down_weight, "row", split_axis=2, concat_axis=1, tiled=True
    )

    logits = jnp.dot(all_features, router, preferred_element_type=jnp.float32)
    onehot = routes[:, :, None] == jnp.arange(expert_count, dtype=jnp.int32)[None, None, :]
    picked = jnp.sum(jnp.where(onehot, logits[:, None, :], 0.0), axis=2)
    raw_exp = jnp.exp(picked)
    gate_weights = raw_exp / jnp.sum(raw_exp, axis=1, keepdims=True)
    share = jax.nn.sigmoid(
        jnp.dot(all_features, shared_gate_vector, preferred_element_type=jnp.float32)
    )
    hit_table = jnp.any(onehot, axis=1).astype(jnp.int32)
    running_count = jnp.cumsum(hit_table, axis=0)
    slot_rank = running_count - hit_table
    route_rank = jnp.sum(jnp.where(onehot, slot_rank[:, None, :], 0), axis=2)
    row_index = routes * capacity + route_rank

    request_ends = jnp.cumsum(lengths[0])
    request_count = lengths.shape[1]
    token_position = jnp.arange(token_count, dtype=jnp.int32)
    request_of = jnp.sum(
        (token_position[:, None] >= request_ends[None, :]).astype(jnp.int32), axis=1
    )
    request_match = request_of[:, None] == jnp.arange(request_count, dtype=jnp.int32)[None, :]
    adapter_of = jnp.sum(jnp.where(request_match, prompt_adapter_index[0][None, :], 0), axis=1)
    low_rank = lax.dot_general(
        all_features, full_in, (((1,), (1,)), ((), ())), preferred_element_type=jnp.float32
    )
    owner = jnp.arange(reduced_rank_value, dtype=jnp.int32) // rank_width
    adapter_mask = adapter_of[:, None] == owner[None, :]
    low_masked = jnp.where(adapter_mask, low_rank.astype(jnp.bfloat16), jnp.zeros((), jnp.bfloat16))
    picked_output_factor = jnp.take(adapter_output_factor, active_adapter_index, axis=0).reshape(
        reduced_rank_value, adapter_output_factor.shape[2]
    )
    adapter_update = jnp.dot(low_masked, picked_output_factor, preferred_element_type=jnp.float32)

    half_width = full_width // 2
    half = row_id % 2
    slot_count = expert_count * capacity
    slot_id = jnp.arange(slot_count, dtype=jnp.int32)
    selection = jnp.any(row_index[None, :, :] == slot_id[:, None, None], axis=2).astype(jnp.bfloat16)
    own_features = lax.dynamic_slice_in_dim(all_features, half * half_width, half_width, axis=1)
    chosen = jnp.dot(selection, own_features, preferred_element_type=jnp.float32).astype(jnp.bfloat16)
    outgoing = chosen.reshape(col_count, local_experts, capacity, half_width)
    own_half = lax.all_to_all(outgoing, "col", split_axis=0, concat_axis=0, tiled=True)
    other_half = lax.ppermute(own_half, "row", [(i, i ^ 1) for i in range(row_count)])

    def half_weights(w, which):
        return lax.dynamic_slice_in_dim(w, which * half_width, half_width, axis=1)

    def project(w):
        return jnp.einsum(
            "sexd,edf->sexf", own_half, half_weights(w, half), preferred_element_type=jnp.float32
        ) + jnp.einsum(
            "sexd,edf->sexf", other_half, half_weights(w, 1 - half), preferred_element_type=jnp.float32
        )

    gate_part = project(routed_gate_weight)
    up_part = project(routed_up_weight)
    hidden = (jax.nn.silu(gate_part) * up_part).astype(jnp.bfloat16)
    hidden_all = lax.all_gather(hidden, "row", axis=3, tiled=True)
    expert_value = jnp.einsum(
        "sexf,efd->sexd", hidden_all, down_by_feature, preferred_element_type=jnp.float32
    )
    returned = lax.all_to_all(expert_value, "col", split_axis=0, concat_axis=0, tiled=True)
    flat_rows = returned.reshape(expert_count * capacity, local_width)
    routed_rows = jnp.take(flat_rows, row_index, axis=0)
    routed = jnp.sum(gate_weights[:, :, None] * routed_rows, axis=1)

    shared_gate_value = jnp.dot(all_features, shared_full[0], preferred_element_type=jnp.float32)
    shared_up_value = jnp.dot(all_features, shared_full[1], preferred_element_type=jnp.float32)
    shared_hidden_units = (
        jax.nn.silu(shared_gate_value) * (shared_up_value + ADAPTER_SCALE * adapter_update)
    ).astype(jnp.bfloat16)
    shared_part = lax.dot_general(
        shared_hidden_units,
        shared_full[2],
        (((1,), (1,)), ((), ())),
        preferred_element_type=jnp.float32,
    )
    shared_part = shared_part * share[:, None]
    shared_sum = lax.psum_scatter(shared_part, "row", scatter_dimension=1, tiled=True)
    return routed + shared_sum


def solution(mesh):
    return jax.shard_map(
        on_device,
        mesh=mesh,
        in_specs=(
            P("col", "row"),
            P(),
            P(),
            P("col", "row"),
            P("col", "row"),
            P("row", "col"),
            P("col", None, "row"),
            P("col", None, "row"),
            P("col", "row", None),
            P(None, None, "row"),
            P(None, None, "row"),
            P("col", None),
            P("col", None),
            P("col", None),
            P(),
        ),
        out_specs=P("col", "row"),
        check_vma=False,
    )
```

```python
import jax
import jax.numpy as jnp
from jax import lax
from jax.sharding import PartitionSpec as P

ADAPTER_SCALE = 2.0


def row_blocks(x, row_count, row_id):
    same_core = [x]
    sources = [row_id]
    for shift in range(2, row_count, 2):
        same_core.append(
            lax.ppermute(x, "row", [(i, (i + shift) % row_count) for i in range(row_count)])
        )
        sources.append((row_id - shift) % row_count)
    own = jnp.stack(same_core)
    other = lax.ppermute(own, "row", [(i, i ^ 1) for i in range(row_count)])
    source = jnp.stack(sources).astype(jnp.int32)
    return jnp.concatenate([own, other]), jnp.concatenate([source, source ^ 1])


def on_device(
    tokens,
    router,
    shared_gate_vector,
    shared_gate_weight,
    shared_up_weight,
    shared_down_weight,
    routed_gate_weight,
    routed_up_weight,
    routed_down_weight,
    adapter_input_factor,
    adapter_output_factor,
    routes,
    lengths,
    prompt_adapter_index,
    active_adapter_index,
):
    row_count = lax.axis_size("row")
    col_count = lax.axis_size("col")
    row_id = lax.axis_index("row")
    token_count = tokens.shape[0]
    local_width = tokens.shape[1]
    picked_input_factor = jnp.take(adapter_input_factor, active_adapter_index, axis=0)
    rank_width = picked_input_factor.shape[1]
    reduced_rank_value = picked_input_factor.shape[0] * rank_width
    blocks, source = row_blocks(
        jnp.concatenate(
            [tokens, picked_input_factor.reshape(reduced_rank_value, local_width)], axis=0
        ),
        row_count,
        row_id,
    )
    row_ids = jnp.arange(row_count, dtype=jnp.int32)
    position = jnp.sum(
        jnp.where(source[None, :] == row_ids[:, None], row_ids[None, :], 0), axis=1
    )
    ordered = jnp.take(blocks, position, axis=0)
    gathered = jnp.transpose(ordered, (1, 0, 2)).reshape(ordered.shape[1], row_count * local_width)
    all_features = gathered[:token_count]
    full_in = gathered[token_count:]
    full_width = all_features.shape[1]
    local_experts = routed_gate_weight.shape[0]
    expert_count = local_experts * col_count
    route_count = routes.shape[1]
    capacity = 2 * token_count * route_count // expert_count

    shared_stack = jnp.stack(
        [shared_gate_weight, shared_up_weight, shared_down_weight.T], axis=0
    )
    shared_full = lax.all_gather(shared_stack, "col", axis=1, tiled=True)

    down_by_feature = lax.all_to_all(
        routed_down_weight, "row", split_axis=2, concat_axis=1, tiled=True
    )

    logits = jnp.dot(all_features, router, preferred_element_type=jnp.float32)
    onehot = routes[:, :, None] == jnp.arange(expert_count, dtype=jnp.int32)[None, None, :]
    picked = jnp.sum(jnp.where(onehot, logits[:, None, :], 0.0), axis=2)
    raw_exp = jnp.exp(picked)
    gate_weights = raw_exp / jnp.sum(raw_exp, axis=1, keepdims=True)
    share = jax.nn.sigmoid(
        jnp.dot(all_features, shared_gate_vector, preferred_element_type=jnp.float32)
    )
    hit_table = jnp.any(onehot, axis=1).astype(jnp.int32)
    running_count = jnp.cumsum(hit_table, axis=0)
    slot_rank = running_count - hit_table
    route_rank = jnp.sum(jnp.where(onehot, slot_rank[:, None, :], 0), axis=2)
    row_index = routes * capacity + route_rank

    request_ends = jnp.cumsum(lengths[0])
    request_count = lengths.shape[1]
    token_position = jnp.arange(token_count, dtype=jnp.int32)
    request_of = jnp.sum(
        (token_position[:, None] >= request_ends[None, :]).astype(jnp.int32), axis=1
    )
    request_match = request_of[:, None] == jnp.arange(request_count, dtype=jnp.int32)[None, :]
    adapter_of = jnp.sum(jnp.where(request_match, prompt_adapter_index[0][None, :], 0), axis=1)
    low_rank = lax.dot_general(
        all_features, full_in, (((1,), (1,)), ((), ())), preferred_element_type=jnp.float32
    )
    owner = jnp.arange(reduced_rank_value, dtype=jnp.int32) // rank_width
    adapter_mask = adapter_of[:, None] == owner[None, :]
    low_masked = jnp.where(adapter_mask, low_rank.astype(jnp.bfloat16), jnp.zeros((), jnp.bfloat16))
    picked_output_factor = jnp.take(adapter_output_factor, active_adapter_index, axis=0).reshape(
        reduced_rank_value, adapter_output_factor.shape[2]
    )
    adapter_update = jnp.dot(low_masked, picked_output_factor, preferred_element_type=jnp.float32)

    half_width = full_width // 2
    half = row_id % 2
    slot_count = expert_count * capacity
    slot_id = jnp.arange(slot_count, dtype=jnp.int32)
    selection = jnp.any(row_index[None, :, :] == slot_id[:, None, None], axis=2).astype(jnp.bfloat16)
    own_features = lax.dynamic_slice_in_dim(all_features, half * half_width, half_width, axis=1)
    chosen = jnp.dot(selection, own_features, preferred_element_type=jnp.float32).astype(jnp.bfloat16)
    outgoing = chosen.reshape(col_count, local_experts, capacity, half_width)
    own_half = lax.all_to_all(outgoing, "col", split_axis=0, concat_axis=0, tiled=True)
    other_half = lax.ppermute(own_half, "row", [(i, i ^ 1) for i in range(row_count)])

    def half_weights(w, which):
        return lax.dynamic_slice_in_dim(w, which * half_width, half_width, axis=1)

    def project(w):
        return jnp.einsum(
            "sexd,edf->sexf", own_half, half_weights(w, half), preferred_element_type=jnp.float32
        ) + jnp.einsum(
            "sexd,edf->sexf", other_half, half_weights(w, 1 - half), preferred_element_type=jnp.float32
        )

    gate_part = project(routed_gate_weight)
    up_part = project(routed_up_weight)
    hidden = (jax.nn.silu(gate_part) * up_part).astype(jnp.bfloat16)
    hidden_blocks, hidden_source = row_blocks(hidden, row_count, row_id)
    local_hidden = hidden.shape[3]
    down_blocks = jnp.take(
        down_by_feature.reshape(local_experts, row_count, local_hidden, local_width),
        hidden_source,
        axis=1,
    )
    expert_value = jnp.einsum(
        "isexf,eifd->sexd", hidden_blocks, down_blocks, preferred_element_type=jnp.float32
    )
    returned = lax.all_to_all(expert_value, "col", split_axis=0, concat_axis=0, tiled=True)
    flat_rows = returned.reshape(expert_count * capacity, local_width)
    routed_rows = jnp.take(flat_rows, row_index, axis=0)
    routed = jnp.sum(gate_weights[:, :, None] * routed_rows, axis=1)

    shared_gate_value = jnp.dot(all_features, shared_full[0], preferred_element_type=jnp.float32)
    shared_up_value = jnp.dot(all_features, shared_full[1], preferred_element_type=jnp.float32)
    shared_hidden_units = (
        jax.nn.silu(shared_gate_value) * (shared_up_value + ADAPTER_SCALE * adapter_update)
    ).astype(jnp.bfloat16)
    shared_part = lax.dot_general(
        shared_hidden_units,
        shared_full[2],
        (((1,), (1,)), ((), ())),
        preferred_element_type=jnp.float32,
    )
    shared_part = shared_part * share[:, None]
    shared_sum = lax.psum_scatter(shared_part, "row", scatter_dimension=1, tiled=True)
    return routed + shared_sum


def solution(mesh):
    return jax.shard_map(
        on_device,
        mesh=mesh,
        in_specs=(
            P("col", "row"),
            P(),
            P(),
            P("col", "row"),
            P("col", "row"),
            P("row", "col"),
            P("col", None, "row"),
            P("col", None, "row"),
            P("col", "row", None),
            P(None, None, "row"),
            P(None, None, "row"),
            P("col", None),
            P("col", None),
            P("col", None),
            P(),
        ),
        out_specs=P("col", "row"),
        check_vma=False,
    )
```

```python
import jax
import jax.numpy as jnp
from jax import lax
from jax.sharding import PartitionSpec as P

ADAPTER_SCALE = 2.0


def on_device(
    tokens,
    router,
    shared_gate_vector,
    shared_gate_weight,
    shared_up_weight,
    shared_down_weight,
    routed_gate_weight,
    routed_up_weight,
    routed_down_weight,
    adapter_input_factor,
    adapter_output_factor,
    routes,
    lengths,
    prompt_adapter_index,
    active_adapter_index,
):
    row_count = lax.axis_size("row")
    col_count = lax.axis_size("col")
    row_id = lax.axis_index("row")
    token_count = tokens.shape[0]
    local_width = tokens.shape[1]
    picked_input_factor = jnp.take(adapter_input_factor, active_adapter_index, axis=0)
    rank_width = picked_input_factor.shape[1]
    reduced_rank_value = picked_input_factor.shape[0] * rank_width
    gathered = lax.all_gather(
        jnp.concatenate(
            [tokens, picked_input_factor.reshape(reduced_rank_value, local_width)], axis=0
        ),
        "row",
        axis=1,
        tiled=True,
    )
    all_features = gathered[:token_count]
    full_in = gathered[token_count:]
    full_width = all_features.shape[1]
    local_experts = routed_gate_weight.shape[0]
    expert_count = local_experts * col_count
    route_count = routes.shape[1]
    capacity = 2 * token_count * route_count // expert_count

    shared_stack = jnp.stack(
        [shared_gate_weight, shared_up_weight, shared_down_weight.T], axis=0
    )
    shared_full = lax.all_gather(shared_stack, "col", axis=1, tiled=True)

    down_by_feature = lax.all_to_all(
        routed_down_weight, "row", split_axis=2, concat_axis=1, tiled=True
    )

    logits = jnp.dot(all_features, router, preferred_element_type=jnp.float32)
    onehot = routes[:, :, None] == jnp.arange(expert_count, dtype=jnp.int32)[None, None, :]
    picked = jnp.sum(jnp.where(onehot, logits[:, None, :], 0.0), axis=2)
    raw_exp = jnp.exp(picked)
    gate_weights = raw_exp / jnp.sum(raw_exp, axis=1, keepdims=True)
    share = jax.nn.sigmoid(
        jnp.dot(all_features, shared_gate_vector, preferred_element_type=jnp.float32)
    )
    hit_table = jnp.any(onehot, axis=1).astype(jnp.int32)
    running_count = jnp.cumsum(hit_table, axis=0)
    slot_rank = running_count - hit_table
    route_rank = jnp.sum(jnp.where(onehot, slot_rank[:, None, :], 0), axis=2)
    row_index = routes * capacity + route_rank

    request_ends = jnp.cumsum(lengths[0])
    request_count = lengths.shape[1]
    token_position = jnp.arange(token_count, dtype=jnp.int32)
    request_of = jnp.sum(
        (token_position[:, None] >= request_ends[None, :]).astype(jnp.int32), axis=1
    )
    request_match = request_of[:, None] == jnp.arange(request_count, dtype=jnp.int32)[None, :]
    adapter_of = jnp.sum(jnp.where(request_match, prompt_adapter_index[0][None, :], 0), axis=1)
    low_rank = lax.dot_general(
        all_features, full_in, (((1,), (1,)), ((), ())), preferred_element_type=jnp.float32
    )
    owner = jnp.arange(reduced_rank_value, dtype=jnp.int32) // rank_width
    adapter_mask = adapter_of[:, None] == owner[None, :]
    low_masked = jnp.where(adapter_mask, low_rank.astype(jnp.bfloat16), jnp.zeros((), jnp.bfloat16))
    picked_output_factor = jnp.take(adapter_output_factor, active_adapter_index, axis=0).reshape(
        reduced_rank_value, adapter_output_factor.shape[2]
    )
    adapter_update = jnp.dot(low_masked, picked_output_factor, preferred_element_type=jnp.float32)

    half_width = full_width // 2
    half = row_id % 2
    slot_count = expert_count * capacity
    slot_id = jnp.arange(slot_count, dtype=jnp.int32)
    selection = jnp.any(row_index[None, :, :] == slot_id[:, None, None], axis=2).astype(jnp.bfloat16)
    own_features = lax.dynamic_slice_in_dim(all_features, half * half_width, half_width, axis=1)
    chosen = jnp.dot(selection, own_features, preferred_element_type=jnp.float32).astype(jnp.bfloat16)
    outgoing = chosen.reshape(col_count, local_experts, capacity, half_width)
    own_half = lax.all_to_all(outgoing, "col", split_axis=0, concat_axis=0, tiled=True)
    other_half = lax.ppermute(own_half, "row", [(i, i ^ 1) for i in range(row_count)])

    def half_weights(w, which):
        return lax.dynamic_slice_in_dim(w, which * half_width, half_width, axis=1)

    def project(w):
        return jnp.einsum(
            "sexd,edf->sexf", own_half, half_weights(w, half), preferred_element_type=jnp.float32
        ) + jnp.einsum(
            "sexd,edf->sexf", other_half, half_weights(w, 1 - half), preferred_element_type=jnp.float32
        )

    gate_part = project(routed_gate_weight)
    up_part = project(routed_up_weight)
    hidden = (jax.nn.silu(gate_part) * up_part).astype(jnp.bfloat16)
    def shifted(x, shift):
        return lax.ppermute(x, "row", [(i, (i + shift) % row_count) for i in range(row_count)])

    def partner(x):
        return lax.ppermute(x, "row", [(i, i ^ 1) for i in range(row_count)])

    local_hidden = hidden.shape[3]
    group_half = hidden.shape[0] // 2
    from_below = shifted(hidden, 2)
    from_above = shifted(hidden, -2)
    far_low = shifted(from_below[:group_half], 2)
    far_high = shifted(from_above[group_half:], -2)
    far = (row_id + 4) % row_count

    def down_of(block, source):
        weight = lax.dynamic_slice_in_dim(down_by_feature, source * local_hidden, local_hidden, axis=1)
        return jnp.einsum("sexf,efd->sexd", block, weight, preferred_element_type=jnp.float32)

    whole_blocks = (
        (hidden, row_id),
        (from_below, (row_id - 2) % row_count),
        (from_above, (row_id + 2) % row_count),
    )
    expert_value = None
    for block, source in whole_blocks:
        for piece, piece_source in ((block, source), (partner(block), source ^ 1)):
            term = down_of(piece, piece_source)
            expert_value = term if expert_value is None else expert_value + term
    low_part = down_of(far_low, far) + down_of(partner(far_low), far ^ 1)
    high_part = down_of(far_high, far) + down_of(partner(far_high), far ^ 1)
    expert_value = expert_value + jnp.concatenate([low_part, high_part], axis=0)
    returned = lax.all_to_all(expert_value, "col", split_axis=0, concat_axis=0, tiled=True)
    flat_rows = returned.reshape(expert_count * capacity, local_width)
    routed_rows = jnp.take(flat_rows, row_index, axis=0)
    routed = jnp.sum(gate_weights[:, :, None] * routed_rows, axis=1)

    shared_gate_value = jnp.dot(all_features, shared_full[0], preferred_element_type=jnp.float32)
    shared_up_value = jnp.dot(all_features, shared_full[1], preferred_element_type=jnp.float32)
    shared_hidden_units = (
        jax.nn.silu(shared_gate_value) * (shared_up_value + ADAPTER_SCALE * adapter_update)
    ).astype(jnp.bfloat16)
    shared_part = lax.dot_general(
        shared_hidden_units,
        shared_full[2],
        (((1,), (1,)), ((), ())),
        preferred_element_type=jnp.float32,
    )
    shared_part = shared_part * share[:, None]
    shared_sum = lax.psum_scatter(shared_part, "row", scatter_dimension=1, tiled=True)
    return routed + shared_sum


def solution(mesh):
    return jax.shard_map(
        on_device,
        mesh=mesh,
        in_specs=(
            P("col", "row"),
            P(),
            P(),
            P("col", "row"),
            P("col", "row"),
            P("row", "col"),
            P("col", None, "row"),
            P("col", None, "row"),
            P("col", "row", None),
            P(None, None, "row"),
            P(None, None, "row"),
            P("col", None),
            P("col", None),
            P("col", None),
            P(),
        ),
        out_specs=P("col", "row"),
        check_vma=False,
    )
```

```python
import jax
import jax.numpy as jnp
from jax import lax
from jax.sharding import PartitionSpec as P

ADAPTER_SCALE = 2.0


def on_device(
    tokens,
    router,
    shared_gate_vector,
    shared_gate_weight,
    shared_up_weight,
    shared_down_weight,
    routed_gate_weight,
    routed_up_weight,
    routed_down_weight,
    adapter_input_factor,
    adapter_output_factor,
    routes,
    lengths,
    prompt_adapter_index,
    active_adapter_index,
):
    row_count = lax.axis_size("row")
    col_count = lax.axis_size("col")
    row_id = lax.axis_index("row")
    token_count = tokens.shape[0]
    local_width = tokens.shape[1]
    picked_input_factor = jnp.take(adapter_input_factor, active_adapter_index, axis=0)
    rank_width = picked_input_factor.shape[1]
    reduced_rank_value = picked_input_factor.shape[0] * rank_width
    gathered = lax.all_gather(
        jnp.concatenate(
            [tokens, picked_input_factor.reshape(reduced_rank_value, local_width)], axis=0
        ),
        "row",
        axis=1,
        tiled=True,
    )
    all_features = gathered[:token_count]
    full_in = gathered[token_count:]
    full_width = all_features.shape[1]
    local_experts = routed_gate_weight.shape[0]
    expert_count = local_experts * col_count
    route_count = routes.shape[1]
    capacity = 2 * token_count * route_count // expert_count

    shared_stack = jnp.stack(
        [shared_gate_weight, shared_up_weight, shared_down_weight.T], axis=0
    )
    shared_full = lax.all_gather(shared_stack, "col", axis=1, tiled=True)


    logits = jnp.dot(all_features, router, preferred_element_type=jnp.float32)
    onehot = routes[:, :, None] == jnp.arange(expert_count, dtype=jnp.int32)[None, None, :]
    picked = jnp.sum(jnp.where(onehot, logits[:, None, :], 0.0), axis=2)
    raw_exp = jnp.exp(picked)
    gate_weights = raw_exp / jnp.sum(raw_exp, axis=1, keepdims=True)
    share = jax.nn.sigmoid(
        jnp.dot(all_features, shared_gate_vector, preferred_element_type=jnp.float32)
    )
    hit_table = jnp.any(onehot, axis=1).astype(jnp.int32)
    running_count = jnp.cumsum(hit_table, axis=0)
    slot_rank = running_count - hit_table
    route_rank = jnp.sum(jnp.where(onehot, slot_rank[:, None, :], 0), axis=2)
    row_index = routes * capacity + route_rank

    request_ends = jnp.cumsum(lengths[0])
    request_count = lengths.shape[1]
    token_position = jnp.arange(token_count, dtype=jnp.int32)
    request_of = jnp.sum(
        (token_position[:, None] >= request_ends[None, :]).astype(jnp.int32), axis=1
    )
    request_match = request_of[:, None] == jnp.arange(request_count, dtype=jnp.int32)[None, :]
    adapter_of = jnp.sum(jnp.where(request_match, prompt_adapter_index[0][None, :], 0), axis=1)
    low_rank = lax.dot_general(
        all_features, full_in, (((1,), (1,)), ((), ())), preferred_element_type=jnp.float32
    )
    owner = jnp.arange(reduced_rank_value, dtype=jnp.int32) // rank_width
    adapter_mask = adapter_of[:, None] == owner[None, :]
    low_masked = jnp.where(adapter_mask, low_rank.astype(jnp.bfloat16), jnp.zeros((), jnp.bfloat16))
    picked_output_factor = jnp.take(adapter_output_factor, active_adapter_index, axis=0).reshape(
        reduced_rank_value, adapter_output_factor.shape[2]
    )
    adapter_update = jnp.dot(low_masked, picked_output_factor, preferred_element_type=jnp.float32)

    half_width = full_width // 2
    half = row_id % 2
    slot_count = expert_count * capacity
    slot_id = jnp.arange(slot_count, dtype=jnp.int32)
    selection = jnp.any(row_index[None, :, :] == slot_id[:, None, None], axis=2).astype(jnp.bfloat16)
    own_features = lax.dynamic_slice_in_dim(all_features, half * half_width, half_width, axis=1)
    chosen = jnp.dot(selection, own_features, preferred_element_type=jnp.float32).astype(jnp.bfloat16)
    outgoing = chosen.reshape(col_count, local_experts, capacity, half_width)
    own_half = lax.all_to_all(outgoing, "col", split_axis=0, concat_axis=0, tiled=True)
    other_half = lax.ppermute(own_half, "row", [(i, i ^ 1) for i in range(row_count)])

    def half_weights(w, which):
        return lax.dynamic_slice_in_dim(w, which * half_width, half_width, axis=1)

    def project(w):
        return jnp.einsum(
            "sexd,edf->sexf", own_half, half_weights(w, half), preferred_element_type=jnp.float32
        ) + jnp.einsum(
            "sexd,edf->sexf", other_half, half_weights(w, 1 - half), preferred_element_type=jnp.float32
        )

    gate_part = project(routed_gate_weight)
    up_part = project(routed_up_weight)
    hidden = (jax.nn.silu(gate_part) * up_part).astype(jnp.bfloat16)
    def shifted(x, shift):
        return lax.ppermute(x, "row", [(i, (i + shift) % row_count) for i in range(row_count)])

    def partner(x):
        return lax.ppermute(x, "row", [(i, i ^ 1) for i in range(row_count)])

    local_hidden = hidden.shape[3]
    group_half = hidden.shape[0] // 2
    from_below = shifted(hidden, 2)
    from_above = shifted(hidden, -2)
    far_low = shifted(from_below[:group_half], 2)
    far_high = shifted(from_above[group_half:], -2)

    def down_slice(k):
        return lax.dynamic_slice_in_dim(
            routed_down_weight, ((row_id + k) % row_count) * local_width, local_width, axis=2
        )

    down_from = [down_slice(0)] + [shifted(down_slice(k), k) for k in range(1, row_count)]
    odd = row_id % 2 == 1

    def down_pick(k_even, k_odd):
        return jnp.where(odd, down_from[k_odd], down_from[k_even])

    def down_of(block, weight):
        return jnp.einsum("sexf,efd->sexd", block, weight, preferred_element_type=jnp.float32)

    whole_blocks = (
        (hidden, down_from[0], down_pick(7, 1)),
        (from_below, down_from[2], down_pick(1, 3)),
        (from_above, down_from[6], down_pick(5, 7)),
    )
    expert_value = None
    for block, weight, partner_weight in whole_blocks:
        term = down_of(block, weight) + down_of(partner(block), partner_weight)
        expert_value = term if expert_value is None else expert_value + term
    far_weight, far_partner_weight = down_from[4], down_pick(3, 5)
    low_part = down_of(far_low, far_weight) + down_of(partner(far_low), far_partner_weight)
    high_part = down_of(far_high, far_weight) + down_of(partner(far_high), far_partner_weight)
    expert_value = expert_value + jnp.concatenate([low_part, high_part], axis=0)
    returned = lax.all_to_all(expert_value, "col", split_axis=0, concat_axis=0, tiled=True)
    flat_rows = returned.reshape(expert_count * capacity, local_width)
    routed_rows = jnp.take(flat_rows, row_index, axis=0)
    routed = jnp.sum(gate_weights[:, :, None] * routed_rows, axis=1)

    shared_gate_value = jnp.dot(all_features, shared_full[0], preferred_element_type=jnp.float32)
    shared_up_value = jnp.dot(all_features, shared_full[1], preferred_element_type=jnp.float32)
    shared_hidden_units = (
        jax.nn.silu(shared_gate_value) * (shared_up_value + ADAPTER_SCALE * adapter_update)
    ).astype(jnp.bfloat16)
    shared_part = lax.dot_general(
        shared_hidden_units,
        shared_full[2],
        (((1,), (1,)), ((), ())),
        preferred_element_type=jnp.float32,
    )
    shared_part = shared_part * share[:, None]
    shared_sum = lax.psum_scatter(shared_part, "row", scatter_dimension=1, tiled=True)
    return routed + shared_sum


def solution(mesh):
    return jax.shard_map(
        on_device,
        mesh=mesh,
        in_specs=(
            P("col", "row"),
            P(),
            P(),
            P("col", "row"),
            P("col", "row"),
            P("row", "col"),
            P("col", None, "row"),
            P("col", None, "row"),
            P("col", "row", None),
            P(None, None, "row"),
            P(None, None, "row"),
            P("col", None),
            P("col", None),
            P("col", None),
            P(),
        ),
        out_specs=P("col", "row"),
        check_vma=False,
    )
```

```python
import jax
import jax.numpy as jnp
from jax import lax
from jax.sharding import PartitionSpec as P

ADAPTER_SCALE = 2.0


def on_device(
    tokens,
    router,
    shared_gate_vector,
    shared_gate_weight,
    shared_up_weight,
    shared_down_weight,
    routed_gate_weight,
    routed_up_weight,
    routed_down_weight,
    adapter_input_factor,
    adapter_output_factor,
    routes,
    lengths,
    prompt_adapter_index,
    active_adapter_index,
):
    row_count = lax.axis_size("row")
    col_count = lax.axis_size("col")
    row_id = lax.axis_index("row")
    token_count = tokens.shape[0]
    local_width = tokens.shape[1]
    picked_input_factor = jnp.take(adapter_input_factor, active_adapter_index, axis=0)
    rank_width = picked_input_factor.shape[1]
    reduced_rank_value = picked_input_factor.shape[0] * rank_width
    gathered = lax.all_gather(
        jnp.concatenate(
            [tokens, picked_input_factor.reshape(reduced_rank_value, local_width)], axis=0
        ),
        "row",
        axis=1,
        tiled=True,
    )
    all_features = gathered[:token_count]
    full_in = gathered[token_count:]
    full_width = all_features.shape[1]
    local_experts = routed_gate_weight.shape[0]
    expert_count = local_experts * col_count
    route_count = routes.shape[1]
    capacity = 2 * token_count * route_count // expert_count

    shared_stack = jnp.stack(
        [shared_gate_weight, shared_up_weight, shared_down_weight.T], axis=0
    )
    shared_full = lax.all_gather(shared_stack, "col", axis=1, tiled=True)


    logits = jnp.dot(all_features, router, preferred_element_type=jnp.float32)
    onehot = routes[:, :, None] == jnp.arange(expert_count, dtype=jnp.int32)[None, None, :]
    picked = jnp.sum(jnp.where(onehot, logits[:, None, :], 0.0), axis=2)
    raw_exp = jnp.exp(picked)
    gate_weights = raw_exp / jnp.sum(raw_exp, axis=1, keepdims=True)
    share = jax.nn.sigmoid(
        jnp.dot(all_features, shared_gate_vector, preferred_element_type=jnp.float32)
    )
    hit_table = jnp.any(onehot, axis=1).astype(jnp.int32)
    running_count = jnp.cumsum(hit_table, axis=0)
    slot_rank = running_count - hit_table
    route_rank = jnp.sum(jnp.where(onehot, slot_rank[:, None, :], 0), axis=2)
    row_index = routes * capacity + route_rank

    request_ends = jnp.cumsum(lengths[0])
    request_count = lengths.shape[1]
    token_position = jnp.arange(token_count, dtype=jnp.int32)
    request_of = jnp.sum(
        (token_position[:, None] >= request_ends[None, :]).astype(jnp.int32), axis=1
    )
    request_match = request_of[:, None] == jnp.arange(request_count, dtype=jnp.int32)[None, :]
    adapter_of = jnp.sum(jnp.where(request_match, prompt_adapter_index[0][None, :], 0), axis=1)
    low_rank = lax.dot_general(
        all_features, full_in, (((1,), (1,)), ((), ())), preferred_element_type=jnp.float32
    )
    owner = jnp.arange(reduced_rank_value, dtype=jnp.int32) // rank_width
    adapter_mask = adapter_of[:, None] == owner[None, :]
    low_masked = jnp.where(adapter_mask, low_rank.astype(jnp.bfloat16), jnp.zeros((), jnp.bfloat16))
    picked_output_factor = jnp.take(adapter_output_factor, active_adapter_index, axis=0).reshape(
        reduced_rank_value, adapter_output_factor.shape[2]
    )
    adapter_update = jnp.dot(low_masked, picked_output_factor, preferred_element_type=jnp.float32)

    half_width = full_width // 2
    half = row_id % 2
    slot_count = expert_count * capacity
    slot_id = jnp.arange(slot_count, dtype=jnp.int32)
    selection = jnp.any(row_index[None, :, :] == slot_id[:, None, None], axis=2).astype(jnp.bfloat16)
    own_features = lax.dynamic_slice_in_dim(all_features, half * half_width, half_width, axis=1)
    chosen = jnp.dot(selection, own_features, preferred_element_type=jnp.float32).astype(jnp.bfloat16)
    outgoing = chosen.reshape(col_count, local_experts, capacity, half_width)
    own_half = lax.all_to_all(outgoing, "col", split_axis=0, concat_axis=0, tiled=True)
    other_half = lax.ppermute(own_half, "row", [(i, i ^ 1) for i in range(row_count)])

    def half_weights(w, which):
        return lax.dynamic_slice_in_dim(w, which * half_width, half_width, axis=1)

    def project(w):
        return jnp.einsum(
            "sexd,edf->sexf", own_half, half_weights(w, half), preferred_element_type=jnp.float32
        ) + jnp.einsum(
            "sexd,edf->sexf", other_half, half_weights(w, 1 - half), preferred_element_type=jnp.float32
        )

    gate_part = project(routed_gate_weight)
    up_part = project(routed_up_weight)
    hidden = (jax.nn.silu(gate_part) * up_part).astype(jnp.bfloat16)
    def shifted(x, shift):
        return lax.ppermute(x, "row", [(i, (i + shift) % row_count) for i in range(row_count)])

    def partner(x):
        return lax.ppermute(x, "row", [(i, i ^ 1) for i in range(row_count)])

    local_hidden = hidden.shape[3]
    group_half = hidden.shape[0] // 2
    from_below = shifted(hidden, 2)
    from_above = shifted(hidden, -2)
    far_low = shifted(from_below[:group_half], 2)
    far_high = shifted(from_above[group_half:], -2)

    def down_slice(k):
        return lax.dynamic_slice_in_dim(
            routed_down_weight, ((row_id + k) % row_count) * local_width, local_width, axis=2
        )

    down_from = [down_slice(0)] + [shifted(down_slice(k), k) for k in range(1, row_count)]
    odd = row_id % 2 == 1

    def down_pick(k_even, k_odd):
        return jnp.where(odd, down_from[k_odd], down_from[k_even])

    def down_of(block, weight):
        return jnp.einsum("sexf,efd->sexd", block, weight, preferred_element_type=jnp.float32)

    whole_blocks = (
        (hidden, down_from[0], down_pick(7, 1)),
        (from_below, down_from[2], down_pick(1, 3)),
        (from_above, down_from[6], down_pick(5, 7)),
    )
    expert_value = None
    for block, weight, partner_weight in whole_blocks:
        term = down_of(block, weight) + down_of(partner(block), partner_weight)
        expert_value = term if expert_value is None else expert_value + term
    far_weight, far_partner_weight = down_from[4], down_pick(3, 5)
    low_part = down_of(far_low, far_weight) + down_of(partner(far_low), far_partner_weight)
    high_part = down_of(far_high, far_weight) + down_of(partner(far_high), far_partner_weight)
    expert_value = expert_value + jnp.concatenate([low_part, high_part], axis=0)
    returned = lax.all_to_all(
        expert_value.astype(jnp.bfloat16), "col", split_axis=0, concat_axis=0, tiled=True
    ).astype(jnp.float32)
    flat_rows = returned.reshape(expert_count * capacity, local_width)
    routed_rows = jnp.take(flat_rows, row_index, axis=0)
    routed = jnp.sum(gate_weights[:, :, None] * routed_rows, axis=1)

    shared_gate_value = jnp.dot(all_features, shared_full[0], preferred_element_type=jnp.float32)
    shared_up_value = jnp.dot(all_features, shared_full[1], preferred_element_type=jnp.float32)
    shared_hidden_units = (
        jax.nn.silu(shared_gate_value) * (shared_up_value + ADAPTER_SCALE * adapter_update)
    ).astype(jnp.bfloat16)
    shared_part = lax.dot_general(
        shared_hidden_units,
        shared_full[2],
        (((1,), (1,)), ((), ())),
        preferred_element_type=jnp.float32,
    )
    shared_part = shared_part * share[:, None]
    shared_sum = lax.psum_scatter(shared_part, "row", scatter_dimension=1, tiled=True)
    return routed + shared_sum


def solution(mesh):
    return jax.shard_map(
        on_device,
        mesh=mesh,
        in_specs=(
            P("col", "row"),
            P(),
            P(),
            P("col", "row"),
            P("col", "row"),
            P("row", "col"),
            P("col", None, "row"),
            P("col", None, "row"),
            P("col", "row", None),
            P(None, None, "row"),
            P(None, None, "row"),
            P("col", None),
            P("col", None),
            P("col", None),
            P(),
        ),
        out_specs=P("col", "row"),
        check_vma=False,
    )
```

```python
import jax
import jax.numpy as jnp
from jax import lax
from jax.sharding import PartitionSpec as P

ADAPTER_SCALE = 2.0


def on_device(
    tokens,
    router,
    shared_gate_vector,
    shared_gate_weight,
    shared_up_weight,
    shared_down_weight,
    routed_gate_weight,
    routed_up_weight,
    routed_down_weight,
    adapter_input_factor,
    adapter_output_factor,
    routes,
    lengths,
    prompt_adapter_index,
    active_adapter_index,
):
    row_count = lax.axis_size("row")
    col_count = lax.axis_size("col")
    row_id = lax.axis_index("row")
    token_count = tokens.shape[0]
    local_width = tokens.shape[1]
    picked_input_factor = jnp.take(adapter_input_factor, active_adapter_index, axis=0)
    rank_width = picked_input_factor.shape[1]
    reduced_rank_value = picked_input_factor.shape[0] * rank_width
    def shifted(x, shift):
        return lax.ppermute(x, "row", [(i, (i + shift) % row_count) for i in range(row_count)])

    def partner(x):
        return lax.ppermute(x, "row", [(i, i ^ 1) for i in range(row_count)])

    pieces = jnp.concatenate(
        [tokens, picked_input_factor.reshape(reduced_rank_value, local_width)], axis=0
    )
    same_parity = [pieces] + [shifted(pieces, shift) for shift in range(2, row_count, 2)]
    other_parity = [partner(piece) for piece in same_parity]
    source = jnp.array([(-shift) % row_count for shift in range(0, row_count, 2)], jnp.int32)
    source = (source + row_id) % row_count
    feature_order = jnp.concatenate([source, source ^ 1])
    own_features = jnp.concatenate([piece[:token_count] for piece in same_parity], axis=1)
    all_features = jnp.concatenate(
        [own_features] + [piece[:token_count] for piece in other_parity], axis=1
    )
    full_in = jnp.concatenate([piece[token_count:] for piece in same_parity + other_parity], axis=1)

    def by_feature_order(w, order, axis):
        blocks = w.reshape(w.shape[:axis] + (row_count, local_width) + w.shape[axis + 1 :])
        picked = jnp.take(blocks, order, axis=axis)
        return picked.reshape(w.shape[:axis] + (-1,) + w.shape[axis + 1 :])

    full_width = all_features.shape[1]
    local_experts = routed_gate_weight.shape[0]
    expert_count = local_experts * col_count
    route_count = routes.shape[1]
    capacity = 2 * token_count * route_count // expert_count

    shared_stack = jnp.stack(
        [shared_gate_weight, shared_up_weight, shared_down_weight.T], axis=0
    )
    shared_full = lax.all_gather(shared_stack, "col", axis=1, tiled=True)


    logits = jnp.dot(
        all_features, by_feature_order(router, feature_order, 0), preferred_element_type=jnp.float32
    )
    onehot = routes[:, :, None] == jnp.arange(expert_count, dtype=jnp.int32)[None, None, :]
    picked = jnp.sum(jnp.where(onehot, logits[:, None, :], 0.0), axis=2)
    raw_exp = jnp.exp(picked)
    gate_weights = raw_exp / jnp.sum(raw_exp, axis=1, keepdims=True)
    share = jax.nn.sigmoid(
        jnp.dot(
            all_features,
            by_feature_order(shared_gate_vector, feature_order, 0),
            preferred_element_type=jnp.float32,
        )
    )
    hit_table = jnp.any(onehot, axis=1).astype(jnp.int32)
    running_count = jnp.cumsum(hit_table, axis=0)
    slot_rank = running_count - hit_table
    route_rank = jnp.sum(jnp.where(onehot, slot_rank[:, None, :], 0), axis=2)
    row_index = routes * capacity + route_rank

    request_ends = jnp.cumsum(lengths[0])
    request_count = lengths.shape[1]
    token_position = jnp.arange(token_count, dtype=jnp.int32)
    request_of = jnp.sum(
        (token_position[:, None] >= request_ends[None, :]).astype(jnp.int32), axis=1
    )
    request_match = request_of[:, None] == jnp.arange(request_count, dtype=jnp.int32)[None, :]
    adapter_of = jnp.sum(jnp.where(request_match, prompt_adapter_index[0][None, :], 0), axis=1)
    low_rank = lax.dot_general(
        all_features, full_in, (((1,), (1,)), ((), ())), preferred_element_type=jnp.float32
    )
    owner = jnp.arange(reduced_rank_value, dtype=jnp.int32) // rank_width
    adapter_mask = adapter_of[:, None] == owner[None, :]
    low_masked = jnp.where(adapter_mask, low_rank.astype(jnp.bfloat16), jnp.zeros((), jnp.bfloat16))
    picked_output_factor = jnp.take(adapter_output_factor, active_adapter_index, axis=0).reshape(
        reduced_rank_value, adapter_output_factor.shape[2]
    )
    adapter_update = jnp.dot(low_masked, picked_output_factor, preferred_element_type=jnp.float32)

    half_width = full_width // 2
    slot_count = expert_count * capacity
    slot_id = jnp.arange(slot_count, dtype=jnp.int32)
    selection = jnp.any(row_index[None, :, :] == slot_id[:, None, None], axis=2).astype(jnp.bfloat16)
    chosen = jnp.dot(selection, own_features, preferred_element_type=jnp.float32).astype(jnp.bfloat16)
    outgoing = chosen.reshape(col_count, local_experts, capacity, half_width)
    own_half = lax.all_to_all(outgoing, "col", split_axis=0, concat_axis=0, tiled=True)
    other_half = lax.ppermute(own_half, "row", [(i, i ^ 1) for i in range(row_count)])

    def project(w):
        return jnp.einsum(
            "sexd,edf->sexf", own_half, by_feature_order(w, source, 1), preferred_element_type=jnp.float32
        ) + jnp.einsum(
            "sexd,edf->sexf", other_half, by_feature_order(w, source ^ 1, 1), preferred_element_type=jnp.float32
        )

    gate_part = project(routed_gate_weight)
    up_part = project(routed_up_weight)
    hidden = (jax.nn.silu(gate_part) * up_part).astype(jnp.bfloat16)

    local_hidden = hidden.shape[3]
    group_half = hidden.shape[0] // 2
    from_below = shifted(hidden, 2)
    from_above = shifted(hidden, -2)
    far_low = shifted(from_below[:group_half], 2)
    far_high = shifted(from_above[group_half:], -2)

    def down_slice(k):
        return lax.dynamic_slice_in_dim(
            routed_down_weight, ((row_id + k) % row_count) * local_width, local_width, axis=2
        )

    down_from = [down_slice(0)] + [shifted(down_slice(k), k) for k in range(1, row_count)]
    odd = row_id % 2 == 1

    def down_pick(k_even, k_odd):
        return jnp.where(odd, down_from[k_odd], down_from[k_even])

    def down_of(block, weight):
        return jnp.einsum("sexf,efd->sexd", block, weight, preferred_element_type=jnp.float32)

    whole_blocks = (
        (hidden, down_from[0], down_pick(7, 1)),
        (from_below, down_from[2], down_pick(1, 3)),
        (from_above, down_from[6], down_pick(5, 7)),
    )
    expert_value = None
    for block, weight, partner_weight in whole_blocks:
        term = down_of(block, weight) + down_of(partner(block), partner_weight)
        expert_value = term if expert_value is None else expert_value + term
    far_weight, far_partner_weight = down_from[4], down_pick(3, 5)
    low_part = down_of(far_low, far_weight) + down_of(partner(far_low), far_partner_weight)
    high_part = down_of(far_high, far_weight) + down_of(partner(far_high), far_partner_weight)
    expert_value = expert_value + jnp.concatenate([low_part, high_part], axis=0)
    returned = lax.all_to_all(expert_value, "col", split_axis=0, concat_axis=0, tiled=True)
    flat_rows = returned.reshape(expert_count * capacity, local_width)
    routed_rows = jnp.take(flat_rows, row_index, axis=0)
    routed = jnp.sum(gate_weights[:, :, None] * routed_rows, axis=1)

    shared_gate_value = jnp.dot(
        all_features, by_feature_order(shared_full[0], feature_order, 0), preferred_element_type=jnp.float32
    )
    shared_up_value = jnp.dot(
        all_features, by_feature_order(shared_full[1], feature_order, 0), preferred_element_type=jnp.float32
    )
    shared_hidden_units = (
        jax.nn.silu(shared_gate_value) * (shared_up_value + ADAPTER_SCALE * adapter_update)
    ).astype(jnp.bfloat16)
    shared_part = lax.dot_general(
        shared_hidden_units,
        shared_full[2],
        (((1,), (1,)), ((), ())),
        preferred_element_type=jnp.float32,
    )
    shared_part = shared_part * share[:, None]
    shared_sum = lax.psum_scatter(shared_part, "row", scatter_dimension=1, tiled=True)
    return routed + shared_sum


def solution(mesh):
    return jax.shard_map(
        on_device,
        mesh=mesh,
        in_specs=(
            P("col", "row"),
            P(),
            P(),
            P("col", "row"),
            P("col", "row"),
            P("row", "col"),
            P("col", None, "row"),
            P("col", None, "row"),
            P("col", "row", None),
            P(None, None, "row"),
            P(None, None, "row"),
            P("col", None),
            P("col", None),
            P("col", None),
            P(),
        ),
        out_specs=P("col", "row"),
        check_vma=False,
    )
```

```python
import jax
import jax.numpy as jnp
from jax import lax
from jax.sharding import PartitionSpec as P

ADAPTER_SCALE = 2.0


def on_device(
    tokens,
    router,
    shared_gate_vector,
    shared_gate_weight,
    shared_up_weight,
    shared_down_weight,
    routed_gate_weight,
    routed_up_weight,
    routed_down_weight,
    adapter_input_factor,
    adapter_output_factor,
    routes,
    lengths,
    prompt_adapter_index,
    active_adapter_index,
):
    row_count = lax.axis_size("row")
    col_count = lax.axis_size("col")
    row_id = lax.axis_index("row")
    token_count = tokens.shape[0]
    local_width = tokens.shape[1]
    picked_input_factor = jnp.take(adapter_input_factor, active_adapter_index, axis=0)
    rank_width = picked_input_factor.shape[1]
    reduced_rank_value = picked_input_factor.shape[0] * rank_width
    gathered = lax.all_gather(
        jnp.concatenate(
            [tokens, picked_input_factor.reshape(reduced_rank_value, local_width)], axis=0
        ),
        "row",
        axis=1,
        tiled=True,
    )
    all_features = gathered[:token_count]
    full_in = gathered[token_count:]
    full_width = all_features.shape[1]
    local_experts = routed_gate_weight.shape[0]
    expert_count = local_experts * col_count
    route_count = routes.shape[1]
    capacity = 2 * token_count * route_count // expert_count

    shared_stack = jnp.stack(
        [shared_gate_weight, shared_up_weight, shared_down_weight.T], axis=0
    )
    shared_full = lax.all_gather(shared_stack, "col", axis=1, tiled=True)


    logits = jnp.dot(all_features, router, preferred_element_type=jnp.float32)
    onehot = routes[:, :, None] == jnp.arange(expert_count, dtype=jnp.int32)[None, None, :]
    picked = jnp.sum(jnp.where(onehot, logits[:, None, :], 0.0), axis=2)
    raw_exp = jnp.exp(picked)
    gate_weights = raw_exp / jnp.sum(raw_exp, axis=1, keepdims=True)
    share = jax.nn.sigmoid(
        jnp.dot(all_features, shared_gate_vector, preferred_element_type=jnp.float32)
    )
    hit_table = jnp.any(onehot, axis=1).astype(jnp.int32)
    running_count = jnp.cumsum(hit_table, axis=0)
    slot_rank = running_count - hit_table
    route_rank = jnp.sum(jnp.where(onehot, slot_rank[:, None, :], 0), axis=2)
    row_index = routes * capacity + route_rank

    request_ends = jnp.cumsum(lengths[0])
    request_count = lengths.shape[1]
    token_position = jnp.arange(token_count, dtype=jnp.int32)
    request_of = jnp.sum(
        (token_position[:, None] >= request_ends[None, :]).astype(jnp.int32), axis=1
    )
    request_match = request_of[:, None] == jnp.arange(request_count, dtype=jnp.int32)[None, :]
    adapter_of = jnp.sum(jnp.where(request_match, prompt_adapter_index[0][None, :], 0), axis=1)
    low_rank = lax.dot_general(
        all_features, full_in, (((1,), (1,)), ((), ())), preferred_element_type=jnp.float32
    )
    owner = jnp.arange(reduced_rank_value, dtype=jnp.int32) // rank_width
    adapter_mask = adapter_of[:, None] == owner[None, :]
    low_masked = jnp.where(adapter_mask, low_rank.astype(jnp.bfloat16), jnp.zeros((), jnp.bfloat16))
    picked_output_factor = jnp.take(adapter_output_factor, active_adapter_index, axis=0).reshape(
        reduced_rank_value, adapter_output_factor.shape[2]
    )
    adapter_update = jnp.dot(low_masked, picked_output_factor, preferred_element_type=jnp.float32)

    half_width = full_width // 2
    half = row_id % 2
    slot_count = expert_count * capacity
    slot_id = jnp.arange(slot_count, dtype=jnp.int32)
    selection = jnp.any(row_index[None, :, :] == slot_id[:, None, None], axis=2).astype(jnp.bfloat16)
    own_features = lax.dynamic_slice_in_dim(all_features, half * half_width, half_width, axis=1)
    chosen = jnp.dot(selection, own_features, preferred_element_type=jnp.float32).astype(jnp.bfloat16)
    def shifted(x, shift):
        return lax.ppermute(x, "row", [(i, (i + shift) % row_count) for i in range(row_count)])

    def partner(x):
        return lax.ppermute(x, "row", [(i, i ^ 1) for i in range(row_count)])

    def down_slice(k):
        return lax.dynamic_slice_in_dim(
            routed_down_weight, ((row_id + k) % row_count) * local_width, local_width, axis=2
        )

    down_from = [down_slice(0)] + [shifted(down_slice(k), k) for k in range(1, row_count)]
    chosen, down_from = lax.optimization_barrier((chosen, down_from))
    outgoing = chosen.reshape(col_count, local_experts, capacity, half_width)
    own_half = lax.all_to_all(outgoing, "col", split_axis=0, concat_axis=0, tiled=True)
    other_half = lax.ppermute(own_half, "row", [(i, i ^ 1) for i in range(row_count)])

    def half_weights(w, which):
        return lax.dynamic_slice_in_dim(w, which * half_width, half_width, axis=1)

    def project(w):
        return jnp.einsum(
            "sexd,edf->sexf", own_half, half_weights(w, half), preferred_element_type=jnp.float32
        ) + jnp.einsum(
            "sexd,edf->sexf", other_half, half_weights(w, 1 - half), preferred_element_type=jnp.float32
        )

    gate_part = project(routed_gate_weight)
    up_part = project(routed_up_weight)
    hidden = (jax.nn.silu(gate_part) * up_part).astype(jnp.bfloat16)
    local_hidden = hidden.shape[3]
    group_half = hidden.shape[0] // 2
    from_below = shifted(hidden, 2)
    from_above = shifted(hidden, -2)
    far_low = shifted(from_below[:group_half], 2)
    far_high = shifted(from_above[group_half:], -2)

    odd = row_id % 2 == 1

    def down_pick(k_even, k_odd):
        return jnp.where(odd, down_from[k_odd], down_from[k_even])

    def down_of(block, weight):
        return jnp.einsum("sexf,efd->sexd", block, weight, preferred_element_type=jnp.float32)

    whole_blocks = (
        (hidden, down_from[0], down_pick(7, 1)),
        (from_below, down_from[2], down_pick(1, 3)),
        (from_above, down_from[6], down_pick(5, 7)),
    )
    expert_value = None
    for block, weight, partner_weight in whole_blocks:
        term = down_of(block, weight) + down_of(partner(block), partner_weight)
        expert_value = term if expert_value is None else expert_value + term
    far_weight, far_partner_weight = down_from[4], down_pick(3, 5)
    low_part = down_of(far_low, far_weight) + down_of(partner(far_low), far_partner_weight)
    high_part = down_of(far_high, far_weight) + down_of(partner(far_high), far_partner_weight)
    expert_value = expert_value + jnp.concatenate([low_part, high_part], axis=0)
    returned = lax.all_to_all(expert_value, "col", split_axis=0, concat_axis=0, tiled=True)
    flat_rows = returned.reshape(expert_count * capacity, local_width)
    routed_rows = jnp.take(flat_rows, row_index, axis=0)
    routed = jnp.sum(gate_weights[:, :, None] * routed_rows, axis=1)

    shared_gate_value = jnp.dot(all_features, shared_full[0], preferred_element_type=jnp.float32)
    shared_up_value = jnp.dot(all_features, shared_full[1], preferred_element_type=jnp.float32)
    shared_hidden_units = (
        jax.nn.silu(shared_gate_value) * (shared_up_value + ADAPTER_SCALE * adapter_update)
    ).astype(jnp.bfloat16)
    shared_part = lax.dot_general(
        shared_hidden_units,
        shared_full[2],
        (((1,), (1,)), ((), ())),
        preferred_element_type=jnp.float32,
    )
    shared_part = shared_part * share[:, None]
    shared_sum = lax.psum_scatter(shared_part, "row", scatter_dimension=1, tiled=True)
    return routed + shared_sum


def solution(mesh):
    return jax.shard_map(
        on_device,
        mesh=mesh,
        in_specs=(
            P("col", "row"),
            P(),
            P(),
            P("col", "row"),
            P("col", "row"),
            P("row", "col"),
            P("col", None, "row"),
            P("col", None, "row"),
            P("col", "row", None),
            P(None, None, "row"),
            P(None, None, "row"),
            P("col", None),
            P("col", None),
            P("col", None),
            P(),
        ),
        out_specs=P("col", "row"),
        check_vma=False,
    )
```

```python
import jax
import jax.numpy as jnp
from jax import lax
from jax.sharding import PartitionSpec as P

ADAPTER_SCALE = 2.0


def on_device(
    tokens,
    router,
    shared_gate_vector,
    shared_gate_weight,
    shared_up_weight,
    shared_down_weight,
    routed_gate_weight,
    routed_up_weight,
    routed_down_weight,
    adapter_input_factor,
    adapter_output_factor,
    routes,
    lengths,
    prompt_adapter_index,
    active_adapter_index,
):
    row_count = lax.axis_size("row")
    col_count = lax.axis_size("col")
    row_id = lax.axis_index("row")
    token_count = tokens.shape[0]
    local_width = tokens.shape[1]
    picked_input_factor = jnp.take(adapter_input_factor, active_adapter_index, axis=0)
    rank_width = picked_input_factor.shape[1]
    reduced_rank_value = picked_input_factor.shape[0] * rank_width
    gathered = lax.all_gather(
        jnp.concatenate(
            [tokens, picked_input_factor.reshape(reduced_rank_value, local_width)], axis=0
        ),
        "row",
        axis=1,
        tiled=True,
    )
    all_features = gathered[:token_count]
    full_in = gathered[token_count:]
    full_width = all_features.shape[1]
    local_experts = routed_gate_weight.shape[0]
    expert_count = local_experts * col_count
    route_count = routes.shape[1]
    capacity = 2 * token_count * route_count // expert_count

    shared_stack = jnp.stack(
        [shared_gate_weight, shared_up_weight, shared_down_weight.T], axis=0
    )
    shared_full = lax.all_gather(shared_stack, "col", axis=1, tiled=True)


    logits = jnp.dot(all_features, router, preferred_element_type=jnp.float32)
    onehot = routes[:, :, None] == jnp.arange(expert_count, dtype=jnp.int32)[None, None, :]
    picked = jnp.sum(jnp.where(onehot, logits[:, None, :], 0.0), axis=2)
    raw_exp = jnp.exp(picked)
    gate_weights = raw_exp / jnp.sum(raw_exp, axis=1, keepdims=True)
    share = jax.nn.sigmoid(
        jnp.dot(all_features, shared_gate_vector, preferred_element_type=jnp.float32)
    )
    hit_table = jnp.any(onehot, axis=1).astype(jnp.int32)
    running_count = jnp.cumsum(hit_table, axis=0)
    slot_rank = running_count - hit_table
    route_rank = jnp.sum(jnp.where(onehot, slot_rank[:, None, :], 0), axis=2)
    row_index = routes * capacity + route_rank

    request_ends = jnp.cumsum(lengths[0])
    request_count = lengths.shape[1]
    token_position = jnp.arange(token_count, dtype=jnp.int32)
    request_of = jnp.sum(
        (token_position[:, None] >= request_ends[None, :]).astype(jnp.int32), axis=1
    )
    request_match = request_of[:, None] == jnp.arange(request_count, dtype=jnp.int32)[None, :]
    adapter_of = jnp.sum(jnp.where(request_match, prompt_adapter_index[0][None, :], 0), axis=1)
    low_rank = lax.dot_general(
        all_features, full_in, (((1,), (1,)), ((), ())), preferred_element_type=jnp.float32
    )
    owner = jnp.arange(reduced_rank_value, dtype=jnp.int32) // rank_width
    adapter_mask = adapter_of[:, None] == owner[None, :]
    low_masked = jnp.where(adapter_mask, low_rank.astype(jnp.bfloat16), jnp.zeros((), jnp.bfloat16))
    picked_output_factor = jnp.take(adapter_output_factor, active_adapter_index, axis=0).reshape(
        reduced_rank_value, adapter_output_factor.shape[2]
    )
    adapter_update = jnp.dot(low_masked, picked_output_factor, preferred_element_type=jnp.float32)

    def shifted(x, shift):
        return lax.ppermute(x, "row", [(i, (i + shift) % row_count) for i in range(row_count)])

    def partner(x):
        return lax.ppermute(x, "row", [(i, i ^ 1) for i in range(row_count)])

    def row_blocks(x):
        group_half = x.shape[0] // 2
        from_below = shifted(x, 2)
        from_above = shifted(x, -2)
        far = jnp.concatenate(
            [shifted(from_below[:group_half], 2), shifted(from_above[group_half:], -2)], axis=0
        )
        same = [x, from_below, from_above, far]
        source = jnp.stack(
            [row_id, (row_id - 2) % row_count, (row_id + 2) % row_count, (row_id + 4) % row_count]
        ).astype(jnp.int32)
        return same + [partner(block) for block in same], jnp.concatenate([source, source ^ 1])

    slot_count = expert_count * capacity
    slot_id = jnp.arange(slot_count, dtype=jnp.int32)
    selection = jnp.any(row_index[None, :, :] == slot_id[:, None, None], axis=2).astype(jnp.bfloat16)
    chosen = jnp.dot(selection, tokens, preferred_element_type=jnp.float32).astype(jnp.bfloat16)
    outgoing = chosen.reshape(col_count, local_experts, capacity, local_width)
    own_block = lax.all_to_all(outgoing, "col", split_axis=0, concat_axis=0, tiled=True)
    slot_blocks, slot_source = row_blocks(own_block)
    slot_features = jnp.concatenate(slot_blocks, axis=3)

    def project(w):
        blocks = w.reshape(w.shape[0], row_count, local_width, w.shape[2])
        ordered = jnp.take(blocks, slot_source, axis=1).reshape(w.shape)
        return jnp.einsum("sexd,edf->sexf", slot_features, ordered, preferred_element_type=jnp.float32)

    gate_part = project(routed_gate_weight)
    up_part = project(routed_up_weight)
    hidden = (jax.nn.silu(gate_part) * up_part).astype(jnp.bfloat16)
    local_hidden = hidden.shape[3]
    group_half = hidden.shape[0] // 2
    from_below = shifted(hidden, 2)
    from_above = shifted(hidden, -2)
    far_low = shifted(from_below[:group_half], 2)
    far_high = shifted(from_above[group_half:], -2)

    def down_slice(k):
        return lax.dynamic_slice_in_dim(
            routed_down_weight, ((row_id + k) % row_count) * local_width, local_width, axis=2
        )

    down_from = [down_slice(0)] + [shifted(down_slice(k), k) for k in range(1, row_count)]
    odd = row_id % 2 == 1

    def down_pick(k_even, k_odd):
        return jnp.where(odd, down_from[k_odd], down_from[k_even])

    def down_of(block, weight):
        return jnp.einsum("sexf,efd->sexd", block, weight, preferred_element_type=jnp.float32)

    whole_blocks = (
        (hidden, down_from[0], down_pick(7, 1)),
        (from_below, down_from[2], down_pick(1, 3)),
        (from_above, down_from[6], down_pick(5, 7)),
    )
    expert_value = None
    for block, weight, partner_weight in whole_blocks:
        term = down_of(block, weight) + down_of(partner(block), partner_weight)
        expert_value = term if expert_value is None else expert_value + term
    far_weight, far_partner_weight = down_from[4], down_pick(3, 5)
    low_part = down_of(far_low, far_weight) + down_of(partner(far_low), far_partner_weight)
    high_part = down_of(far_high, far_weight) + down_of(partner(far_high), far_partner_weight)
    expert_value = expert_value + jnp.concatenate([low_part, high_part], axis=0)
    returned = lax.all_to_all(expert_value, "col", split_axis=0, concat_axis=0, tiled=True)
    flat_rows = returned.reshape(expert_count * capacity, local_width)
    routed_rows = jnp.take(flat_rows, row_index, axis=0)
    routed = jnp.sum(gate_weights[:, :, None] * routed_rows, axis=1)

    shared_gate_value = jnp.dot(all_features, shared_full[0], preferred_element_type=jnp.float32)
    shared_up_value = jnp.dot(all_features, shared_full[1], preferred_element_type=jnp.float32)
    shared_hidden_units = (
        jax.nn.silu(shared_gate_value) * (shared_up_value + ADAPTER_SCALE * adapter_update)
    ).astype(jnp.bfloat16)
    shared_part = lax.dot_general(
        shared_hidden_units,
        shared_full[2],
        (((1,), (1,)), ((), ())),
        preferred_element_type=jnp.float32,
    )
    shared_part = shared_part * share[:, None]
    shared_sum = lax.psum_scatter(shared_part, "row", scatter_dimension=1, tiled=True)
    return routed + shared_sum


def solution(mesh):
    return jax.shard_map(
        on_device,
        mesh=mesh,
        in_specs=(
            P("col", "row"),
            P(),
            P(),
            P("col", "row"),
            P("col", "row"),
            P("row", "col"),
            P("col", None, "row"),
            P("col", None, "row"),
            P("col", "row", None),
            P(None, None, "row"),
            P(None, None, "row"),
            P("col", None),
            P("col", None),
            P("col", None),
            P(),
        ),
        out_specs=P("col", "row"),
        check_vma=False,
    )
```

```python
import jax
import jax.numpy as jnp
from jax import lax
from jax.sharding import PartitionSpec as P

ADAPTER_SCALE = 2.0


def on_device(
    tokens,
    router,
    shared_gate_vector,
    shared_gate_weight,
    shared_up_weight,
    shared_down_weight,
    routed_gate_weight,
    routed_up_weight,
    routed_down_weight,
    adapter_input_factor,
    adapter_output_factor,
    routes,
    lengths,
    prompt_adapter_index,
    active_adapter_index,
):
    row_count = lax.axis_size("row")
    col_count = lax.axis_size("col")
    row_id = lax.axis_index("row")
    token_count = tokens.shape[0]
    local_width = tokens.shape[1]
    picked_input_factor = jnp.take(adapter_input_factor, active_adapter_index, axis=0)
    rank_width = picked_input_factor.shape[1]
    reduced_rank_value = picked_input_factor.shape[0] * rank_width
    gathered = lax.all_gather(
        jnp.concatenate(
            [tokens, picked_input_factor.reshape(reduced_rank_value, local_width)], axis=0
        ),
        "row",
        axis=1,
        tiled=True,
    )
    all_features = gathered[:token_count]
    full_in = gathered[token_count:]
    full_width = all_features.shape[1]
    local_experts = routed_gate_weight.shape[0]
    expert_count = local_experts * col_count
    route_count = routes.shape[1]
    capacity = 2 * token_count * route_count // expert_count

    shared_stack = jnp.stack(
        [shared_gate_weight, shared_up_weight, shared_down_weight.T], axis=0
    )
    shared_full = lax.all_gather(shared_stack, "col", axis=1, tiled=True)


    logits = jnp.dot(all_features, router, preferred_element_type=jnp.float32)
    onehot = routes[:, :, None] == jnp.arange(expert_count, dtype=jnp.int32)[None, None, :]
    picked = jnp.sum(jnp.where(onehot, logits[:, None, :], 0.0), axis=2)
    raw_exp = jnp.exp(picked)
    gate_weights = raw_exp / jnp.sum(raw_exp, axis=1, keepdims=True)
    share = jax.nn.sigmoid(
        jnp.dot(all_features, shared_gate_vector, preferred_element_type=jnp.float32)
    )
    hit_table = jnp.any(onehot, axis=1).astype(jnp.int32)
    running_count = jnp.cumsum(hit_table, axis=0)
    slot_rank = running_count - hit_table
    route_rank = jnp.sum(jnp.where(onehot, slot_rank[:, None, :], 0), axis=2)
    row_index = routes * capacity + route_rank

    request_ends = jnp.cumsum(lengths[0])
    request_count = lengths.shape[1]
    token_position = jnp.arange(token_count, dtype=jnp.int32)
    request_of = jnp.sum(
        (token_position[:, None] >= request_ends[None, :]).astype(jnp.int32), axis=1
    )
    request_match = request_of[:, None] == jnp.arange(request_count, dtype=jnp.int32)[None, :]
    adapter_of = jnp.sum(jnp.where(request_match, prompt_adapter_index[0][None, :], 0), axis=1)
    low_rank = lax.dot_general(
        all_features, full_in, (((1,), (1,)), ((), ())), preferred_element_type=jnp.float32
    )
    owner = jnp.arange(reduced_rank_value, dtype=jnp.int32) // rank_width
    adapter_mask = adapter_of[:, None] == owner[None, :]
    low_masked = jnp.where(adapter_mask, low_rank.astype(jnp.bfloat16), jnp.zeros((), jnp.bfloat16))
    picked_output_factor = jnp.take(adapter_output_factor, active_adapter_index, axis=0).reshape(
        reduced_rank_value, adapter_output_factor.shape[2]
    )
    adapter_update = jnp.dot(low_masked, picked_output_factor, preferred_element_type=jnp.float32)

    def shifted(x, shift):
        return lax.ppermute(x, "row", [(i, (i + shift) % row_count) for i in range(row_count)])

    def partner(x):
        return lax.ppermute(x, "row", [(i, i ^ 1) for i in range(row_count)])

    def row_blocks(x):
        group_half = x.shape[0] // 2
        from_below = shifted(x, 2)
        from_above = shifted(x, -2)
        far = jnp.concatenate(
            [shifted(from_below[:group_half], 2), shifted(from_above[group_half:], -2)], axis=0
        )
        same = [x, from_below, from_above, far]
        source = jnp.stack(
            [row_id, (row_id - 2) % row_count, (row_id + 2) % row_count, (row_id + 4) % row_count]
        ).astype(jnp.int32)
        return same + [partner(block) for block in same], jnp.concatenate([source, source ^ 1])

    slot_count = expert_count * capacity
    slot_id = jnp.arange(slot_count, dtype=jnp.int32)
    selection = jnp.any(row_index[None, :, :] == slot_id[:, None, None], axis=2).astype(jnp.bfloat16)
    chosen = jnp.dot(selection, tokens, preferred_element_type=jnp.float32).astype(jnp.bfloat16)
    outgoing = chosen.reshape(col_count, local_experts, capacity, local_width)
    own_block = lax.all_to_all(outgoing, "col", split_axis=0, concat_axis=0, tiled=True)
    slot_blocks, slot_source = row_blocks(own_block)
    slot_features = jnp.concatenate(slot_blocks, axis=3)

    def project(w):
        blocks = w.reshape(w.shape[0], row_count, local_width, w.shape[2])
        ordered = jnp.take(blocks, slot_source, axis=1).reshape(w.shape)
        return jnp.einsum("sexd,edf->sexf", slot_features, ordered, preferred_element_type=jnp.float32)

    gate_part = project(routed_gate_weight)
    up_part = project(routed_up_weight)
    hidden = (jax.nn.silu(gate_part) * up_part).astype(jnp.bfloat16)
    local_hidden = hidden.shape[3]
    group_half = hidden.shape[0] // 2
    from_below = shifted(hidden, 2)
    from_above = shifted(hidden, -2)
    shared_gate_value = jnp.dot(all_features, shared_full[0], preferred_element_type=jnp.float32)
    shared_up_value = jnp.dot(all_features, shared_full[1], preferred_element_type=jnp.float32)
    shared_hidden_units = (
        jax.nn.silu(shared_gate_value) * (shared_up_value + ADAPTER_SCALE * adapter_update)
    ).astype(jnp.bfloat16)
    shared_part = lax.dot_general(
        shared_hidden_units,
        shared_full[2],
        (((1,), (1,)), ((), ())),
        preferred_element_type=jnp.float32,
    )
    shared_part = shared_part * share[:, None]
    shared_part, from_below, from_above = lax.optimization_barrier((shared_part, from_below, from_above))
    shared_sum = lax.psum_scatter(shared_part, "row", scatter_dimension=1, tiled=True)
    far_low = shifted(from_below[:group_half], 2)
    far_high = shifted(from_above[group_half:], -2)

    def down_slice(k):
        return lax.dynamic_slice_in_dim(
            routed_down_weight, ((row_id + k) % row_count) * local_width, local_width, axis=2
        )

    down_from = [down_slice(0)] + [shifted(down_slice(k), k) for k in range(1, row_count)]
    odd = row_id % 2 == 1

    def down_pick(k_even, k_odd):
        return jnp.where(odd, down_from[k_odd], down_from[k_even])

    def down_of(block, weight):
        return jnp.einsum("sexf,efd->sexd", block, weight, preferred_element_type=jnp.float32)

    whole_blocks = (
        (hidden, down_from[0], down_pick(7, 1)),
        (from_below, down_from[2], down_pick(1, 3)),
        (from_above, down_from[6], down_pick(5, 7)),
    )
    expert_value = None
    for block, weight, partner_weight in whole_blocks:
        term = down_of(block, weight) + down_of(partner(block), partner_weight)
        expert_value = term if expert_value is None else expert_value + term
    far_weight, far_partner_weight = down_from[4], down_pick(3, 5)
    low_part = down_of(far_low, far_weight) + down_of(partner(far_low), far_partner_weight)
    high_part = down_of(far_high, far_weight) + down_of(partner(far_high), far_partner_weight)
    expert_value = expert_value + jnp.concatenate([low_part, high_part], axis=0)
    returned = lax.all_to_all(expert_value, "col", split_axis=0, concat_axis=0, tiled=True)
    flat_rows = returned.reshape(expert_count * capacity, local_width)
    routed_rows = jnp.take(flat_rows, row_index, axis=0)
    routed = jnp.sum(gate_weights[:, :, None] * routed_rows, axis=1)

    return routed + shared_sum


def solution(mesh):
    return jax.shard_map(
        on_device,
        mesh=mesh,
        in_specs=(
            P("col", "row"),
            P(),
            P(),
            P("col", "row"),
            P("col", "row"),
            P("row", "col"),
            P("col", None, "row"),
            P("col", None, "row"),
            P("col", "row", None),
            P(None, None, "row"),
            P(None, None, "row"),
            P("col", None),
            P("col", None),
            P("col", None),
            P(),
        ),
        out_specs=P("col", "row"),
        check_vma=False,
    )
```

```python
import jax
import jax.numpy as jnp
from jax import lax
from jax.sharding import PartitionSpec as P

ADAPTER_SCALE = 2.0


def on_device(
    tokens,
    router,
    shared_gate_vector,
    shared_gate_weight,
    shared_up_weight,
    shared_down_weight,
    routed_gate_weight,
    routed_up_weight,
    routed_down_weight,
    adapter_input_factor,
    adapter_output_factor,
    routes,
    lengths,
    prompt_adapter_index,
    active_adapter_index,
):
    row_count = lax.axis_size("row")
    col_count = lax.axis_size("col")
    row_id = lax.axis_index("row")
    token_count = tokens.shape[0]
    local_width = tokens.shape[1]
    picked_input_factor = jnp.take(adapter_input_factor, active_adapter_index, axis=0)
    rank_width = picked_input_factor.shape[1]
    reduced_rank_value = picked_input_factor.shape[0] * rank_width
    gathered = lax.all_gather(
        jnp.concatenate(
            [tokens, picked_input_factor.reshape(reduced_rank_value, local_width)], axis=0
        ),
        "row",
        axis=1,
        tiled=True,
    )
    all_features = gathered[:token_count]
    full_in = gathered[token_count:]
    full_width = all_features.shape[1]
    local_experts = routed_gate_weight.shape[0]
    expert_count = local_experts * col_count
    route_count = routes.shape[1]
    capacity = 2 * token_count * route_count // expert_count

    shared_stack = jnp.stack(
        [shared_gate_weight, shared_up_weight, shared_down_weight.T], axis=0
    )
    shared_full = lax.all_gather(shared_stack, "col", axis=1, tiled=True)


    logits = jnp.dot(all_features, router, preferred_element_type=jnp.float32)
    onehot = routes[:, :, None] == jnp.arange(expert_count, dtype=jnp.int32)[None, None, :]
    picked = jnp.sum(jnp.where(onehot, logits[:, None, :], 0.0), axis=2)
    raw_exp = jnp.exp(picked)
    gate_weights = raw_exp / jnp.sum(raw_exp, axis=1, keepdims=True)
    share = jax.nn.sigmoid(
        jnp.dot(all_features, shared_gate_vector, preferred_element_type=jnp.float32)
    )
    hit_table = jnp.any(onehot, axis=1).astype(jnp.int32)
    running_count = jnp.cumsum(hit_table, axis=0)
    slot_rank = running_count - hit_table
    route_rank = jnp.sum(jnp.where(onehot, slot_rank[:, None, :], 0), axis=2)
    row_index = routes * capacity + route_rank

    request_ends = jnp.cumsum(lengths[0])
    request_count = lengths.shape[1]
    token_position = jnp.arange(token_count, dtype=jnp.int32)
    request_of = jnp.sum(
        (token_position[:, None] >= request_ends[None, :]).astype(jnp.int32), axis=1
    )
    request_match = request_of[:, None] == jnp.arange(request_count, dtype=jnp.int32)[None, :]
    adapter_of = jnp.sum(jnp.where(request_match, prompt_adapter_index[0][None, :], 0), axis=1)
    low_rank = lax.dot_general(
        all_features, full_in, (((1,), (1,)), ((), ())), preferred_element_type=jnp.float32
    )
    owner = jnp.arange(reduced_rank_value, dtype=jnp.int32) // rank_width
    adapter_mask = adapter_of[:, None] == owner[None, :]
    low_masked = jnp.where(adapter_mask, low_rank.astype(jnp.bfloat16), jnp.zeros((), jnp.bfloat16))
    picked_output_factor = jnp.take(adapter_output_factor, active_adapter_index, axis=0).reshape(
        reduced_rank_value, adapter_output_factor.shape[2]
    )
    adapter_update = jnp.dot(low_masked, picked_output_factor, preferred_element_type=jnp.float32)

    def shifted(x, shift):
        return lax.ppermute(x, "row", [(i, (i + shift) % row_count) for i in range(row_count)])

    def partner(x):
        return lax.ppermute(x, "row", [(i, i ^ 1) for i in range(row_count)])

    def row_blocks(x):
        group_half = x.shape[0] // 2
        from_below = shifted(x, 2)
        from_above = shifted(x, -2)
        far = jnp.concatenate(
            [shifted(from_below[:group_half], 2), shifted(from_above[group_half:], -2)], axis=0
        )
        same = [x, from_below, from_above, far]
        source = jnp.stack(
            [row_id, (row_id - 2) % row_count, (row_id + 2) % row_count, (row_id + 4) % row_count]
        ).astype(jnp.int32)
        return same + [partner(block) for block in same], jnp.concatenate([source, source ^ 1])

    slot_count = expert_count * capacity
    slot_id = jnp.arange(slot_count, dtype=jnp.int32)
    selection = jnp.any(row_index[None, :, :] == slot_id[:, None, None], axis=2).astype(jnp.bfloat16)
    chosen = jnp.dot(selection, tokens, preferred_element_type=jnp.float32).astype(jnp.bfloat16)
    outgoing = chosen.reshape(col_count, local_experts, capacity, local_width)
    own_block = lax.all_to_all(outgoing, "col", split_axis=0, concat_axis=0, tiled=True)
    slot_blocks, slot_source = row_blocks(own_block)
    slot_features = jnp.concatenate(slot_blocks, axis=3)

    def project(w):
        blocks = w.reshape(w.shape[0], row_count, local_width, w.shape[2])
        ordered = jnp.take(blocks, slot_source, axis=1).reshape(w.shape)
        return jnp.einsum("sexd,edf->sexf", slot_features, ordered, preferred_element_type=jnp.float32)

    gate_part = project(routed_gate_weight)
    up_part = project(routed_up_weight)
    hidden = (jax.nn.silu(gate_part) * up_part).astype(jnp.bfloat16)
    local_hidden = hidden.shape[3]
    group_half = hidden.shape[0] // 2
    from_below = shifted(hidden, 2)
    from_above = shifted(hidden, -2)
    shared_gate_value = jnp.dot(all_features, shared_full[0], preferred_element_type=jnp.float32)
    shared_up_value = jnp.dot(all_features, shared_full[1], preferred_element_type=jnp.float32)
    shared_hidden_units = (
        jax.nn.silu(shared_gate_value) * (shared_up_value + ADAPTER_SCALE * adapter_update)
    ).astype(jnp.bfloat16)
    shared_part = lax.dot_general(
        shared_hidden_units,
        shared_full[2],
        (((1,), (1,)), ((), ())),
        preferred_element_type=jnp.float32,
    )
    shared_part = shared_part * share[:, None]
    shared_part, from_below, from_above = lax.optimization_barrier((shared_part, from_below, from_above))
    shared_sum = lax.psum_scatter(shared_part, "row", scatter_dimension=1, tiled=True)
    far_low = shifted(from_below[:group_half], 2)
    far_high = shifted(from_above[group_half:], -2)

    def down_slice(k):
        return lax.dynamic_slice_in_dim(
            routed_down_weight, ((row_id + k) % row_count) * local_width, local_width, axis=2
        )

    down_from = [down_slice(0)] + [shifted(down_slice(k), k) for k in range(1, row_count)]
    odd = row_id % 2 == 1

    def down_pick(k_even, k_odd):
        return jnp.where(odd, down_from[k_odd], down_from[k_even])

    def down_of(block, weight):
        return jnp.einsum("sexf,efd->sexd", block, weight, preferred_element_type=jnp.float32)

    whole_blocks = (
        (hidden, down_from[0], down_pick(7, 1)),
        (from_below, down_from[2], down_pick(1, 3)),
        (from_above, down_from[6], down_pick(5, 7)),
    )
    expert_value = None
    for block, weight, partner_weight in whole_blocks:
        term = down_of(block, weight) + down_of(partner(block), partner_weight)
        expert_value = term if expert_value is None else expert_value + term
    far_weight, far_partner_weight = down_from[4], down_pick(3, 5)
    low_part = down_of(far_low, far_weight) + down_of(partner(far_low), far_partner_weight)
    high_part = down_of(far_high, far_weight) + down_of(partner(far_high), far_partner_weight)
    expert_value = expert_value + jnp.concatenate([low_part, high_part], axis=0)
    returned = lax.all_to_all(
        expert_value.astype(jnp.bfloat16), "col", split_axis=0, concat_axis=0, tiled=True
    ).astype(jnp.float32)
    flat_rows = returned.reshape(expert_count * capacity, local_width)
    routed_rows = jnp.take(flat_rows, row_index, axis=0)
    routed = jnp.sum(gate_weights[:, :, None] * routed_rows, axis=1)

    return routed + shared_sum


def solution(mesh):
    return jax.shard_map(
        on_device,
        mesh=mesh,
        in_specs=(
            P("col", "row"),
            P(),
            P(),
            P("col", "row"),
            P("col", "row"),
            P("row", "col"),
            P("col", None, "row"),
            P("col", None, "row"),
            P("col", "row", None),
            P(None, None, "row"),
            P(None, None, "row"),
            P("col", None),
            P("col", None),
            P("col", None),
            P(),
        ),
        out_specs=P("col", "row"),
        check_vma=False,
    )
```

```python
import jax
import jax.numpy as jnp
from jax import lax
from jax.sharding import PartitionSpec as P

ADAPTER_SCALE = 2.0


def on_device(
    tokens,
    router,
    shared_gate_vector,
    shared_gate_weight,
    shared_up_weight,
    shared_down_weight,
    routed_gate_weight,
    routed_up_weight,
    routed_down_weight,
    adapter_input_factor,
    adapter_output_factor,
    routes,
    lengths,
    prompt_adapter_index,
    active_adapter_index,
):
    row_count = lax.axis_size("row")
    col_count = lax.axis_size("col")
    row_id = lax.axis_index("row")
    token_count = tokens.shape[0]
    local_width = tokens.shape[1]
    picked_input_factor = jnp.take(adapter_input_factor, active_adapter_index, axis=0)
    rank_width = picked_input_factor.shape[1]
    reduced_rank_value = picked_input_factor.shape[0] * rank_width
    gathered = lax.all_gather(
        jnp.concatenate(
            [tokens, picked_input_factor.reshape(reduced_rank_value, local_width)], axis=0
        ),
        "row",
        axis=1,
        tiled=True,
    )
    all_features = gathered[:token_count]
    full_in = gathered[token_count:]
    full_width = all_features.shape[1]
    local_experts = routed_gate_weight.shape[0]
    expert_count = local_experts * col_count
    route_count = routes.shape[1]
    capacity = 2 * token_count * route_count // expert_count

    shared_stack = jnp.stack(
        [shared_gate_weight, shared_up_weight, shared_down_weight.T], axis=0
    )
    shared_full = lax.all_gather(shared_stack, "col", axis=1, tiled=True)


    logits = jnp.dot(all_features, router, preferred_element_type=jnp.float32)
    onehot = routes[:, :, None] == jnp.arange(expert_count, dtype=jnp.int32)[None, None, :]
    picked = jnp.sum(jnp.where(onehot, logits[:, None, :], 0.0), axis=2)
    raw_exp = jnp.exp(picked)
    gate_weights = raw_exp / jnp.sum(raw_exp, axis=1, keepdims=True)
    share = jax.nn.sigmoid(
        jnp.dot(all_features, shared_gate_vector, preferred_element_type=jnp.float32)
    )
    hit_table = jnp.any(onehot, axis=1).astype(jnp.int32)
    running_count = jnp.cumsum(hit_table, axis=0)
    slot_rank = running_count - hit_table
    route_rank = jnp.sum(jnp.where(onehot, slot_rank[:, None, :], 0), axis=2)
    row_index = routes * capacity + route_rank

    request_ends = jnp.cumsum(lengths[0])
    request_count = lengths.shape[1]
    token_position = jnp.arange(token_count, dtype=jnp.int32)
    request_of = jnp.sum(
        (token_position[:, None] >= request_ends[None, :]).astype(jnp.int32), axis=1
    )
    request_match = request_of[:, None] == jnp.arange(request_count, dtype=jnp.int32)[None, :]
    adapter_of = jnp.sum(jnp.where(request_match, prompt_adapter_index[0][None, :], 0), axis=1)
    low_rank = lax.dot_general(
        all_features, full_in, (((1,), (1,)), ((), ())), preferred_element_type=jnp.float32
    )
    owner = jnp.arange(reduced_rank_value, dtype=jnp.int32) // rank_width
    adapter_mask = adapter_of[:, None] == owner[None, :]
    low_masked = jnp.where(adapter_mask, low_rank.astype(jnp.bfloat16), jnp.zeros((), jnp.bfloat16))
    picked_output_factor = jnp.take(adapter_output_factor, active_adapter_index, axis=0).reshape(
        reduced_rank_value, adapter_output_factor.shape[2]
    )
    adapter_update = jnp.dot(low_masked, picked_output_factor, preferred_element_type=jnp.float32)

    def shifted(x, shift):
        return lax.ppermute(x, "row", [(i, (i + shift) % row_count) for i in range(row_count)])

    def partner(x):
        return lax.ppermute(x, "row", [(i, i ^ 1) for i in range(row_count)])

    def row_blocks(x, tie=None):
        group_half = x.shape[0] // 2
        from_below = shifted(x, 2)
        from_above = shifted(x, -2)
        if tie is not None:
            tie, from_below, from_above = lax.optimization_barrier((tie, from_below, from_above))
        far = jnp.concatenate(
            [shifted(from_below[:group_half], 2), shifted(from_above[group_half:], -2)], axis=0
        )
        same = [x, from_below, from_above, far]
        swapped = partner(jnp.stack(same))
        source = jnp.stack(
            [row_id, (row_id - 2) % row_count, (row_id + 2) % row_count, (row_id + 4) % row_count]
        ).astype(jnp.int32)
        blocks = same + [swapped[j] for j in range(len(same))]
        return blocks, jnp.concatenate([source, source ^ 1]), tie

    slot_count = expert_count * capacity
    slot_id = jnp.arange(slot_count, dtype=jnp.int32)
    selection = jnp.any(row_index[None, :, :] == slot_id[:, None, None], axis=2).astype(jnp.bfloat16)
    chosen = jnp.dot(selection, tokens, preferred_element_type=jnp.float32).astype(jnp.bfloat16)
    outgoing = chosen.reshape(col_count, local_experts, capacity, local_width)
    own_block = lax.all_to_all(outgoing, "col", split_axis=0, concat_axis=0, tiled=True)
    slot_blocks, slot_source, _ = row_blocks(own_block)
    slot_features = jnp.concatenate(slot_blocks, axis=3)

    def project(w):
        blocks = w.reshape(w.shape[0], row_count, local_width, w.shape[2])
        ordered = jnp.take(blocks, slot_source, axis=1).reshape(w.shape)
        return jnp.einsum("sexd,edf->sexf", slot_features, ordered, preferred_element_type=jnp.float32)

    gate_part = project(routed_gate_weight)
    up_part = project(routed_up_weight)
    hidden = (jax.nn.silu(gate_part) * up_part).astype(jnp.bfloat16)
    shared_gate_value = jnp.dot(all_features, shared_full[0], preferred_element_type=jnp.float32)
    shared_up_value = jnp.dot(all_features, shared_full[1], preferred_element_type=jnp.float32)
    shared_hidden_units = (
        jax.nn.silu(shared_gate_value) * (shared_up_value + ADAPTER_SCALE * adapter_update)
    ).astype(jnp.bfloat16)
    shared_part = lax.dot_general(
        shared_hidden_units,
        shared_full[2],
        (((1,), (1,)), ((), ())),
        preferred_element_type=jnp.float32,
    )
    shared_part = shared_part * share[:, None]
    hidden_blocks, _, shared_part = row_blocks(hidden, tie=shared_part)
    shared_sum = lax.psum_scatter(shared_part, "row", scatter_dimension=1, tiled=True)
    def down_slice(k):
        return lax.dynamic_slice_in_dim(
            routed_down_weight, ((row_id + k) % row_count) * local_width, local_width, axis=2
        )

    down_from = [down_slice(0)] + [shifted(down_slice(k), k) for k in range(1, row_count)]
    odd = row_id % 2 == 1

    def down_pick(k_even, k_odd):
        return jnp.where(odd, down_from[k_odd], down_from[k_even])

    hidden_weights = [
        down_from[0], down_from[2], down_from[6], down_from[4],
        down_pick(7, 1), down_pick(1, 3), down_pick(5, 7), down_pick(3, 5),
    ]
    expert_value = jnp.einsum(
        "sexf,efd->sexd",
        jnp.concatenate(hidden_blocks, axis=3),
        jnp.concatenate(hidden_weights, axis=1),
        preferred_element_type=jnp.float32,
    )
    returned = lax.all_to_all(
        expert_value.astype(jnp.bfloat16), "col", split_axis=0, concat_axis=0, tiled=True
    ).astype(jnp.float32)
    flat_rows = returned.reshape(expert_count * capacity, local_width)
    routed_rows = jnp.take(flat_rows, row_index, axis=0)
    routed = jnp.sum(gate_weights[:, :, None] * routed_rows, axis=1)

    return routed + shared_sum


def solution(mesh):
    return jax.shard_map(
        on_device,
        mesh=mesh,
        in_specs=(
            P("col", "row"),
            P(),
            P(),
            P("col", "row"),
            P("col", "row"),
            P("row", "col"),
            P("col", None, "row"),
            P("col", None, "row"),
            P("col", "row", None),
            P(None, None, "row"),
            P(None, None, "row"),
            P("col", None),
            P("col", None),
            P("col", None),
            P(),
        ),
        out_specs=P("col", "row"),
        check_vma=False,
    )
```

```python
import jax
import jax.numpy as jnp
from jax import lax
from jax.sharding import PartitionSpec as P

ADAPTER_SCALE = 2.0


def on_device(
    tokens,
    router,
    shared_gate_vector,
    shared_gate_weight,
    shared_up_weight,
    shared_down_weight,
    routed_gate_weight,
    routed_up_weight,
    routed_down_weight,
    adapter_input_factor,
    adapter_output_factor,
    routes,
    lengths,
    prompt_adapter_index,
    active_adapter_index,
):
    row_count = lax.axis_size("row")
    col_count = lax.axis_size("col")
    row_id = lax.axis_index("row")
    token_count = tokens.shape[0]
    local_width = tokens.shape[1]
    picked_input_factor = jnp.take(adapter_input_factor, active_adapter_index, axis=0)
    rank_width = picked_input_factor.shape[1]
    reduced_rank_value = picked_input_factor.shape[0] * rank_width
    gathered = lax.all_gather(
        jnp.concatenate(
            [tokens, picked_input_factor.reshape(reduced_rank_value, local_width)], axis=0
        ),
        "row",
        axis=1,
        tiled=True,
    )
    all_features = gathered[:token_count]
    full_in = gathered[token_count:]
    full_width = all_features.shape[1]
    local_experts = routed_gate_weight.shape[0]
    expert_count = local_experts * col_count
    route_count = routes.shape[1]
    capacity = 2 * token_count * route_count // expert_count

    shared_stack = jnp.stack(
        [shared_gate_weight, shared_up_weight, shared_down_weight.T], axis=0
    )
    shared_full = lax.all_gather(shared_stack, "col", axis=1, tiled=True)


    logits = jnp.dot(all_features, router, preferred_element_type=jnp.float32)
    onehot = routes[:, :, None] == jnp.arange(expert_count, dtype=jnp.int32)[None, None, :]
    picked = jnp.sum(jnp.where(onehot, logits[:, None, :], 0.0), axis=2)
    raw_exp = jnp.exp(picked)
    gate_weights = raw_exp / jnp.sum(raw_exp, axis=1, keepdims=True)
    share = jax.nn.sigmoid(
        jnp.dot(all_features, shared_gate_vector, preferred_element_type=jnp.float32)
    )
    hit_table = jnp.any(onehot, axis=1).astype(jnp.int32)
    running_count = jnp.cumsum(hit_table, axis=0)
    slot_rank = running_count - hit_table
    route_rank = jnp.sum(jnp.where(onehot, slot_rank[:, None, :], 0), axis=2)
    row_index = routes * capacity + route_rank

    request_ends = jnp.cumsum(lengths[0])
    request_count = lengths.shape[1]
    token_position = jnp.arange(token_count, dtype=jnp.int32)
    request_of = jnp.sum(
        (token_position[:, None] >= request_ends[None, :]).astype(jnp.int32), axis=1
    )
    request_match = request_of[:, None] == jnp.arange(request_count, dtype=jnp.int32)[None, :]
    adapter_of = jnp.sum(jnp.where(request_match, prompt_adapter_index[0][None, :], 0), axis=1)
    low_rank = lax.dot_general(
        all_features, full_in, (((1,), (1,)), ((), ())), preferred_element_type=jnp.float32
    )
    owner = jnp.arange(reduced_rank_value, dtype=jnp.int32) // rank_width
    adapter_mask = adapter_of[:, None] == owner[None, :]
    low_masked = jnp.where(adapter_mask, low_rank.astype(jnp.bfloat16), jnp.zeros((), jnp.bfloat16))
    picked_output_factor = jnp.take(adapter_output_factor, active_adapter_index, axis=0).reshape(
        reduced_rank_value, adapter_output_factor.shape[2]
    )
    adapter_update = jnp.dot(low_masked, picked_output_factor, preferred_element_type=jnp.float32)

    def shifted(x, shift):
        return lax.ppermute(x, "row", [(i, (i + shift) % row_count) for i in range(row_count)])

    def partner(x):
        return lax.ppermute(x, "row", [(i, i ^ 1) for i in range(row_count)])

    def row_blocks(x):
        group_half = x.shape[0] // 2
        from_below = shifted(x, 2)
        from_above = shifted(x, -2)
        far = jnp.concatenate(
            [shifted(from_below[:group_half], 2), shifted(from_above[group_half:], -2)], axis=0
        )
        same = [x, from_below, from_above, far]
        source = jnp.stack(
            [row_id, (row_id - 2) % row_count, (row_id + 2) % row_count, (row_id + 4) % row_count]
        ).astype(jnp.int32)
        return same + [partner(block) for block in same], jnp.concatenate([source, source ^ 1])

    slot_count = expert_count * capacity
    slot_id = jnp.arange(slot_count, dtype=jnp.int32)
    selection = jnp.any(row_index[None, :, :] == slot_id[:, None, None], axis=2).astype(jnp.bfloat16)
    chosen = jnp.dot(selection, tokens, preferred_element_type=jnp.float32).astype(jnp.bfloat16)
    outgoing = chosen.reshape(col_count, local_experts, capacity, local_width)
    own_block = lax.all_to_all(outgoing, "col", split_axis=0, concat_axis=0, tiled=True)
    slot_blocks, slot_source = row_blocks(own_block)
    slot_features = jnp.concatenate(slot_blocks, axis=3)

    def project(w):
        blocks = w.reshape(w.shape[0], row_count, local_width, w.shape[2])
        ordered = jnp.take(blocks, slot_source, axis=1).reshape(w.shape)
        return jnp.einsum("sexd,edf->sexf", slot_features, ordered, preferred_element_type=jnp.float32)

    gate_up = project(jnp.concatenate([routed_gate_weight, routed_up_weight], axis=2))
    gate_part = gate_up[..., : routed_gate_weight.shape[2]]
    up_part = gate_up[..., routed_gate_weight.shape[2] :]
    hidden = (jax.nn.silu(gate_part) * up_part).astype(jnp.bfloat16)
    local_hidden = hidden.shape[3]
    group_half = hidden.shape[0] // 2
    from_below = shifted(hidden, 2)
    from_above = shifted(hidden, -2)
    shared_gate_value = jnp.dot(all_features, shared_full[0], preferred_element_type=jnp.float32)
    shared_up_value = jnp.dot(all_features, shared_full[1], preferred_element_type=jnp.float32)
    shared_hidden_units = (
        jax.nn.silu(shared_gate_value) * (shared_up_value + ADAPTER_SCALE * adapter_update)
    ).astype(jnp.bfloat16)
    shared_part = lax.dot_general(
        shared_hidden_units,
        shared_full[2],
        (((1,), (1,)), ((), ())),
        preferred_element_type=jnp.float32,
    )
    shared_part = shared_part * share[:, None]
    shared_part, from_below, from_above = lax.optimization_barrier((shared_part, from_below, from_above))
    shared_sum = lax.psum_scatter(shared_part, "row", scatter_dimension=1, tiled=True)
    far_low = shifted(from_below[:group_half], 2)
    far_high = shifted(from_above[group_half:], -2)

    def down_slice(k):
        return lax.dynamic_slice_in_dim(
            routed_down_weight, ((row_id + k) % row_count) * local_width, local_width, axis=2
        )

    down_from = [down_slice(0)] + [shifted(down_slice(k), k) for k in range(1, row_count)]
    odd = row_id % 2 == 1

    def down_pick(k_even, k_odd):
        return jnp.where(odd, down_from[k_odd], down_from[k_even])

    def down_of(block, weight):
        return jnp.einsum("sexf,efd->sexd", block, weight, preferred_element_type=jnp.float32)

    whole_blocks = (
        (hidden, down_from[0], down_pick(7, 1)),
        (from_below, down_from[2], down_pick(1, 3)),
        (from_above, down_from[6], down_pick(5, 7)),
    )
    expert_value = None
    for block, weight, partner_weight in whole_blocks:
        term = down_of(block, weight) + down_of(partner(block), partner_weight)
        expert_value = term if expert_value is None else expert_value + term
    far_weight, far_partner_weight = down_from[4], down_pick(3, 5)
    low_part = down_of(far_low, far_weight) + down_of(partner(far_low), far_partner_weight)
    high_part = down_of(far_high, far_weight) + down_of(partner(far_high), far_partner_weight)
    expert_value = expert_value + jnp.concatenate([low_part, high_part], axis=0)
    returned = lax.all_to_all(
        expert_value.astype(jnp.bfloat16), "col", split_axis=0, concat_axis=0, tiled=True
    )
    flat_rows = returned.reshape(expert_count * capacity, local_width)
    routed = None
    for k in range(route_count):
        pick = (row_index[:, k][:, None] == slot_id[None, :]).astype(jnp.bfloat16)
        row = jnp.dot(pick, flat_rows, preferred_element_type=jnp.float32)
        term = gate_weights[:, k][:, None] * row
        routed = term if routed is None else routed + term

    return routed + shared_sum


def solution(mesh):
    return jax.shard_map(
        on_device,
        mesh=mesh,
        in_specs=(
            P("col", "row"),
            P(),
            P(),
            P("col", "row"),
            P("col", "row"),
            P("row", "col"),
            P("col", None, "row"),
            P("col", None, "row"),
            P("col", "row", None),
            P(None, None, "row"),
            P(None, None, "row"),
            P("col", None),
            P("col", None),
            P("col", None),
            P(),
        ),
        out_specs=P("col", "row"),
        check_vma=False,
    )
```

```python
import jax
import jax.numpy as jnp
from jax import lax
from jax.sharding import PartitionSpec as P

ADAPTER_SCALE = 2.0


def on_device(
    tokens,
    router,
    shared_gate_vector,
    shared_gate_weight,
    shared_up_weight,
    shared_down_weight,
    routed_gate_weight,
    routed_up_weight,
    routed_down_weight,
    adapter_input_factor,
    adapter_output_factor,
    routes,
    lengths,
    prompt_adapter_index,
    active_adapter_index,
):
    row_count = lax.axis_size("row")
    col_count = lax.axis_size("col")
    row_id = lax.axis_index("row")
    token_count = tokens.shape[0]
    local_width = tokens.shape[1]
    picked_input_factor = jnp.take(adapter_input_factor, active_adapter_index, axis=0)
    rank_width = picked_input_factor.shape[1]
    reduced_rank_value = picked_input_factor.shape[0] * rank_width
    gathered = lax.all_gather(
        jnp.concatenate(
            [tokens, picked_input_factor.reshape(reduced_rank_value, local_width)], axis=0
        ),
        "row",
        axis=1,
        tiled=True,
    )
    all_features = gathered[:token_count]
    full_in = gathered[token_count:]
    full_width = all_features.shape[1]
    local_experts = routed_gate_weight.shape[0]
    expert_count = local_experts * col_count
    route_count = routes.shape[1]
    capacity = 2 * token_count * route_count // expert_count

    shared_stack = jnp.stack(
        [shared_gate_weight, shared_up_weight, shared_down_weight.T], axis=0
    )
    shared_full = lax.all_gather(shared_stack, "col", axis=1, tiled=True)


    logits = jnp.dot(all_features, router, preferred_element_type=jnp.float32)
    onehot = routes[:, :, None] == jnp.arange(expert_count, dtype=jnp.int32)[None, None, :]
    picked = jnp.sum(jnp.where(onehot, logits[:, None, :], 0.0), axis=2)
    raw_exp = jnp.exp(picked)
    gate_weights = raw_exp / jnp.sum(raw_exp, axis=1, keepdims=True)
    share = jax.nn.sigmoid(
        jnp.dot(all_features, shared_gate_vector, preferred_element_type=jnp.float32)
    )
    hit_table = jnp.any(onehot, axis=1).astype(jnp.int32)
    running_count = jnp.cumsum(hit_table, axis=0)
    slot_rank = running_count - hit_table
    route_rank = jnp.sum(jnp.where(onehot, slot_rank[:, None, :], 0), axis=2)
    row_index = routes * capacity + route_rank

    request_ends = jnp.cumsum(lengths[0])
    request_count = lengths.shape[1]
    token_position = jnp.arange(token_count, dtype=jnp.int32)
    request_of = jnp.sum(
        (token_position[:, None] >= request_ends[None, :]).astype(jnp.int32), axis=1
    )
    request_match = request_of[:, None] == jnp.arange(request_count, dtype=jnp.int32)[None, :]
    adapter_of = jnp.sum(jnp.where(request_match, prompt_adapter_index[0][None, :], 0), axis=1)
    low_rank = lax.dot_general(
        all_features, full_in, (((1,), (1,)), ((), ())), preferred_element_type=jnp.float32
    )
    owner = jnp.arange(reduced_rank_value, dtype=jnp.int32) // rank_width
    adapter_mask = adapter_of[:, None] == owner[None, :]
    low_masked = jnp.where(adapter_mask, low_rank.astype(jnp.bfloat16), jnp.zeros((), jnp.bfloat16))
    picked_output_factor = jnp.take(adapter_output_factor, active_adapter_index, axis=0).reshape(
        reduced_rank_value, adapter_output_factor.shape[2]
    )
    adapter_update = jnp.dot(low_masked, picked_output_factor, preferred_element_type=jnp.float32)

    def shifted(x, shift):
        return lax.ppermute(x, "row", [(i, (i + shift) % row_count) for i in range(row_count)])

    def partner(x):
        return lax.ppermute(x, "row", [(i, i ^ 1) for i in range(row_count)])

    def row_blocks(x):
        group_half = x.shape[0] // 2
        from_below = shifted(x, 2)
        from_above = shifted(x, -2)
        far = jnp.concatenate(
            [shifted(from_below[:group_half], 2), shifted(from_above[group_half:], -2)], axis=0
        )
        same = [x, from_below, from_above, far]
        source = jnp.stack(
            [row_id, (row_id - 2) % row_count, (row_id + 2) % row_count, (row_id + 4) % row_count]
        ).astype(jnp.int32)
        return same + [partner(block) for block in same], jnp.concatenate([source, source ^ 1])

    slot_count = expert_count * capacity
    slot_id = jnp.arange(slot_count, dtype=jnp.int32)
    selection = jnp.any(row_index[None, :, :] == slot_id[:, None, None], axis=2).astype(jnp.bfloat16)
    chosen = jnp.dot(selection, tokens, preferred_element_type=jnp.float32).astype(jnp.bfloat16)
    outgoing = chosen.reshape(col_count, local_experts, capacity, local_width)
    own_block = lax.all_to_all(outgoing, "col", split_axis=0, concat_axis=0, tiled=True)
    slot_blocks, slot_source = row_blocks(own_block)
    arrival_groups = ((0, 4, 1, 2), (5, 6, 3, 7))

    def project(w):
        blocks = w.reshape(w.shape[0], row_count, local_width, w.shape[2])
        total = None
        for group in arrival_groups:
            features = jnp.concatenate([slot_blocks[j] for j in group], axis=3)
            order = jnp.stack([slot_source[j] for j in group])
            ordered = jnp.take(blocks, order, axis=1).reshape(w.shape[0], -1, w.shape[2])
            term = jnp.einsum("sexd,edf->sexf", features, ordered, preferred_element_type=jnp.float32)
            total = term if total is None else total + term
        return total

    gate_up = project(jnp.concatenate([routed_gate_weight, routed_up_weight], axis=2))
    gate_part = gate_up[..., : routed_gate_weight.shape[2]]
    up_part = gate_up[..., routed_gate_weight.shape[2] :]
    hidden = (jax.nn.silu(gate_part) * up_part).astype(jnp.bfloat16)
    local_hidden = hidden.shape[3]
    group_half = hidden.shape[0] // 2
    from_below = shifted(hidden, 2)
    from_above = shifted(hidden, -2)
    shared_gate_value = jnp.dot(all_features, shared_full[0], preferred_element_type=jnp.float32)
    shared_up_value = jnp.dot(all_features, shared_full[1], preferred_element_type=jnp.float32)
    shared_hidden_units = (
        jax.nn.silu(shared_gate_value) * (shared_up_value + ADAPTER_SCALE * adapter_update)
    ).astype(jnp.bfloat16)
    shared_part = lax.dot_general(
        shared_hidden_units,
        shared_full[2],
        (((1,), (1,)), ((), ())),
        preferred_element_type=jnp.float32,
    )
    shared_part = shared_part * share[:, None]
    shared_part, from_below, from_above = lax.optimization_barrier((shared_part, from_below, from_above))
    shared_sum = lax.psum_scatter(shared_part, "row", scatter_dimension=1, tiled=True)
    far_low = shifted(from_below[:group_half], 2)
    far_high = shifted(from_above[group_half:], -2)

    def down_slice(k):
        return lax.dynamic_slice_in_dim(
            routed_down_weight, ((row_id + k) % row_count) * local_width, local_width, axis=2
        )

    down_from = [down_slice(0)] + [shifted(down_slice(k), k) for k in range(1, row_count)]
    odd = row_id % 2 == 1

    def down_pick(k_even, k_odd):
        return jnp.where(odd, down_from[k_odd], down_from[k_even])

    def down_of(block, weight):
        return jnp.einsum("sexf,efd->sexd", block, weight, preferred_element_type=jnp.float32)

    whole_blocks = (
        (hidden, down_from[0], down_pick(7, 1)),
        (from_below, down_from[2], down_pick(1, 3)),
        (from_above, down_from[6], down_pick(5, 7)),
    )
    expert_value = None
    for block, weight, partner_weight in whole_blocks:
        term = down_of(block, weight) + down_of(partner(block), partner_weight)
        expert_value = term if expert_value is None else expert_value + term
    far_weight, far_partner_weight = down_from[4], down_pick(3, 5)
    low_part = down_of(far_low, far_weight) + down_of(partner(far_low), far_partner_weight)
    high_part = down_of(far_high, far_weight) + down_of(partner(far_high), far_partner_weight)
    expert_value = expert_value + jnp.concatenate([low_part, high_part], axis=0)
    returned = lax.all_to_all(
        expert_value.astype(jnp.bfloat16), "col", split_axis=0, concat_axis=0, tiled=True
    )
    flat_rows = returned.reshape(expert_count * capacity, local_width)
    routed = None
    for k in range(route_count):
        pick = (row_index[:, k][:, None] == slot_id[None, :]).astype(jnp.bfloat16)
        row = jnp.dot(pick, flat_rows, preferred_element_type=jnp.float32)
        term = gate_weights[:, k][:, None] * row
        routed = term if routed is None else routed + term

    return routed + shared_sum


def solution(mesh):
    return jax.shard_map(
        on_device,
        mesh=mesh,
        in_specs=(
            P("col", "row"),
            P(),
            P(),
            P("col", "row"),
            P("col", "row"),
            P("row", "col"),
            P("col", None, "row"),
            P("col", None, "row"),
            P("col", "row", None),
            P(None, None, "row"),
            P(None, None, "row"),
            P("col", None),
            P("col", None),
            P("col", None),
            P(),
        ),
        out_specs=P("col", "row"),
        check_vma=False,
    )
```

```python
import jax
import jax.numpy as jnp
from jax import lax
from jax.sharding import PartitionSpec as P

ADAPTER_SCALE = 2.0


def on_device(
    tokens,
    router,
    shared_gate_vector,
    shared_gate_weight,
    shared_up_weight,
    shared_down_weight,
    routed_gate_weight,
    routed_up_weight,
    routed_down_weight,
    adapter_input_factor,
    adapter_output_factor,
    routes,
    lengths,
    prompt_adapter_index,
    active_adapter_index,
):
    row_count = lax.axis_size("row")
    col_count = lax.axis_size("col")
    row_id = lax.axis_index("row")
    token_count = tokens.shape[0]
    local_width = tokens.shape[1]
    picked_input_factor = jnp.take(adapter_input_factor, active_adapter_index, axis=0)
    rank_width = picked_input_factor.shape[1]
    reduced_rank_value = picked_input_factor.shape[0] * rank_width
    gathered = lax.all_gather(
        jnp.concatenate(
            [tokens, picked_input_factor.reshape(reduced_rank_value, local_width)], axis=0
        ),
        "row",
        axis=1,
        tiled=True,
    )
    all_features = gathered[:token_count]
    full_in = gathered[token_count:]
    full_width = all_features.shape[1]
    local_experts = routed_gate_weight.shape[0]
    expert_count = local_experts * col_count
    route_count = routes.shape[1]
    capacity = 2 * token_count * route_count // expert_count

    shared_stack = jnp.stack(
        [shared_gate_weight, shared_up_weight, shared_down_weight.T], axis=0
    )
    shared_full = lax.all_gather(shared_stack, "col", axis=1, tiled=True)


    logits = jnp.dot(all_features, router, preferred_element_type=jnp.float32)
    onehot = routes[:, :, None] == jnp.arange(expert_count, dtype=jnp.int32)[None, None, :]
    picked = jnp.sum(jnp.where(onehot, logits[:, None, :], 0.0), axis=2)
    raw_exp = jnp.exp(picked)
    gate_weights = raw_exp / jnp.sum(raw_exp, axis=1, keepdims=True)
    share = jax.nn.sigmoid(
        jnp.dot(all_features, shared_gate_vector, preferred_element_type=jnp.float32)
    )
    hit_table = jnp.any(onehot, axis=1).astype(jnp.int32)
    running_count = jnp.cumsum(hit_table, axis=0)
    slot_rank = running_count - hit_table
    route_rank = jnp.sum(jnp.where(onehot, slot_rank[:, None, :], 0), axis=2)
    row_index = routes * capacity + route_rank

    request_ends = jnp.cumsum(lengths[0])
    request_count = lengths.shape[1]
    token_position = jnp.arange(token_count, dtype=jnp.int32)
    request_of = jnp.sum(
        (token_position[:, None] >= request_ends[None, :]).astype(jnp.int32), axis=1
    )
    request_match = request_of[:, None] == jnp.arange(request_count, dtype=jnp.int32)[None, :]
    adapter_of = jnp.sum(jnp.where(request_match, prompt_adapter_index[0][None, :], 0), axis=1)
    low_rank = lax.dot_general(
        all_features, full_in, (((1,), (1,)), ((), ())), preferred_element_type=jnp.float32
    )
    owner = jnp.arange(reduced_rank_value, dtype=jnp.int32) // rank_width
    adapter_mask = adapter_of[:, None] == owner[None, :]
    low_masked = jnp.where(adapter_mask, low_rank.astype(jnp.bfloat16), jnp.zeros((), jnp.bfloat16))
    picked_output_factor = jnp.take(adapter_output_factor, active_adapter_index, axis=0).reshape(
        reduced_rank_value, adapter_output_factor.shape[2]
    )
    adapter_update = jnp.dot(low_masked, picked_output_factor, preferred_element_type=jnp.float32)

    def shifted(x, shift):
        return lax.ppermute(x, "row", [(i, (i + shift) % row_count) for i in range(row_count)])

    def partner(x):
        return lax.ppermute(x, "row", [(i, i ^ 1) for i in range(row_count)])

    def row_blocks(x):
        group_half = x.shape[0] // 2
        from_below = shifted(x, 2)
        from_above = shifted(x, -2)
        far = jnp.concatenate(
            [shifted(from_below[:group_half], 2), shifted(from_above[group_half:], -2)], axis=0
        )
        same = [x, from_below, from_above, far]
        source = jnp.stack(
            [row_id, (row_id - 2) % row_count, (row_id + 2) % row_count, (row_id + 4) % row_count]
        ).astype(jnp.int32)
        return same + [partner(block) for block in same], jnp.concatenate([source, source ^ 1])

    slot_count = expert_count * capacity
    slot_id = jnp.arange(slot_count, dtype=jnp.int32)
    selection = jnp.any(row_index[None, :, :] == slot_id[:, None, None], axis=2).astype(jnp.bfloat16)
    chosen = jnp.dot(selection, tokens, preferred_element_type=jnp.float32).astype(jnp.bfloat16)
    outgoing = chosen.reshape(col_count, local_experts, capacity, local_width)
    own_block = lax.all_to_all(outgoing, "col", split_axis=0, concat_axis=0, tiled=True)
    slot_blocks, slot_source = row_blocks(own_block)
    arrival_groups = ((0, 4, 1, 2), (5, 6, 3, 7))

    def project(w):
        blocks = w.reshape(w.shape[0], row_count, local_width, w.shape[2])
        total = None
        for group in arrival_groups:
            features = jnp.concatenate([slot_blocks[j] for j in group], axis=3)
            order = jnp.stack([slot_source[j] for j in group])
            ordered = jnp.take(blocks, order, axis=1).reshape(w.shape[0], -1, w.shape[2])
            term = jnp.einsum("sexd,edf->sexf", features, ordered, preferred_element_type=jnp.float32)
            total = term if total is None else total + term
        return total

    gate_up = project(jnp.concatenate([routed_gate_weight, routed_up_weight], axis=2))
    gate_part = gate_up[..., : routed_gate_weight.shape[2]]
    up_part = gate_up[..., routed_gate_weight.shape[2] :]
    hidden = (jax.nn.silu(gate_part) * up_part).astype(jnp.bfloat16)
    local_hidden = hidden.shape[3]
    group_half = hidden.shape[0] // 2
    from_below = shifted(hidden, 2)
    from_above = shifted(hidden, -2)
    shared_gate_value = jnp.dot(all_features, shared_full[0], preferred_element_type=jnp.float32)
    shared_up_value = jnp.dot(all_features, shared_full[1], preferred_element_type=jnp.float32)
    shared_hidden_units = (
        jax.nn.silu(shared_gate_value) * (shared_up_value + ADAPTER_SCALE * adapter_update)
    ).astype(jnp.bfloat16)
    shared_part = lax.dot_general(
        shared_hidden_units,
        shared_full[2],
        (((1,), (1,)), ((), ())),
        preferred_element_type=jnp.float32,
    )
    shared_part = shared_part * share[:, None]
    far_low = shifted(from_below[:group_half], 2)
    far_high = shifted(from_above[group_half:], -2)
    shared_part, far_low, far_high = lax.optimization_barrier((shared_part, far_low, far_high))
    shared_sum = lax.psum_scatter(shared_part, "row", scatter_dimension=1, tiled=True)

    def down_slice(k):
        return lax.dynamic_slice_in_dim(
            routed_down_weight, ((row_id + k) % row_count) * local_width, local_width, axis=2
        )

    down_from = [down_slice(0)] + [shifted(down_slice(k), k) for k in range(1, row_count)]
    odd = row_id % 2 == 1

    def down_pick(k_even, k_odd):
        return jnp.where(odd, down_from[k_odd], down_from[k_even])

    def down_of(block, weight):
        return jnp.einsum("sexf,efd->sexd", block, weight, preferred_element_type=jnp.float32)

    whole_blocks = (
        (hidden, down_from[0], down_pick(7, 1)),
        (from_below, down_from[2], down_pick(1, 3)),
        (from_above, down_from[6], down_pick(5, 7)),
    )
    expert_value = None
    for block, weight, partner_weight in whole_blocks:
        term = down_of(block, weight) + down_of(partner(block), partner_weight)
        expert_value = term if expert_value is None else expert_value + term
    far_weight, far_partner_weight = down_from[4], down_pick(3, 5)
    low_part = down_of(far_low, far_weight) + down_of(partner(far_low), far_partner_weight)
    high_part = down_of(far_high, far_weight) + down_of(partner(far_high), far_partner_weight)
    expert_value = expert_value + jnp.concatenate([low_part, high_part], axis=0)
    returned = lax.all_to_all(
        expert_value.astype(jnp.bfloat16), "col", split_axis=0, concat_axis=0, tiled=True
    )
    flat_rows = returned.reshape(expert_count * capacity, local_width)
    routed = None
    for k in range(route_count):
        pick = (row_index[:, k][:, None] == slot_id[None, :]).astype(jnp.bfloat16)
        row = jnp.dot(pick, flat_rows, preferred_element_type=jnp.float32)
        term = gate_weights[:, k][:, None] * row
        routed = term if routed is None else routed + term

    return routed + shared_sum


def solution(mesh):
    return jax.shard_map(
        on_device,
        mesh=mesh,
        in_specs=(
            P("col", "row"),
            P(),
            P(),
            P("col", "row"),
            P("col", "row"),
            P("row", "col"),
            P("col", None, "row"),
            P("col", None, "row"),
            P("col", "row", None),
            P(None, None, "row"),
            P(None, None, "row"),
            P("col", None),
            P("col", None),
            P("col", None),
            P(),
        ),
        out_specs=P("col", "row"),
        check_vma=False,
    )
```

```python
import jax
import jax.numpy as jnp
from jax import lax
from jax.sharding import PartitionSpec as P

ADAPTER_SCALE = 2.0


def on_device(
    tokens,
    router,
    shared_gate_vector,
    shared_gate_weight,
    shared_up_weight,
    shared_down_weight,
    routed_gate_weight,
    routed_up_weight,
    routed_down_weight,
    adapter_input_factor,
    adapter_output_factor,
    routes,
    lengths,
    prompt_adapter_index,
    active_adapter_index,
):
    row_count = lax.axis_size("row")
    col_count = lax.axis_size("col")
    row_id = lax.axis_index("row")
    token_count = tokens.shape[0]
    local_width = tokens.shape[1]
    picked_input_factor = jnp.take(adapter_input_factor, active_adapter_index, axis=0)
    rank_width = picked_input_factor.shape[1]
    reduced_rank_value = picked_input_factor.shape[0] * rank_width
    gathered = lax.all_gather(
        jnp.concatenate(
            [tokens, picked_input_factor.reshape(reduced_rank_value, local_width)], axis=0
        ),
        "row",
        axis=1,
        tiled=True,
    )
    all_features = gathered[:token_count]
    full_in = gathered[token_count:]
    full_width = all_features.shape[1]
    local_experts = routed_gate_weight.shape[0]
    expert_count = local_experts * col_count
    route_count = routes.shape[1]
    capacity = 2 * token_count * route_count // expert_count

    shared_stack = jnp.stack(
        [shared_gate_weight, shared_up_weight, shared_down_weight.T], axis=0
    )
    shared_full = lax.all_gather(shared_stack, "col", axis=1, tiled=True)


    logits = jnp.dot(all_features, router, preferred_element_type=jnp.float32)
    onehot = routes[:, :, None] == jnp.arange(expert_count, dtype=jnp.int32)[None, None, :]
    picked = jnp.sum(jnp.where(onehot, logits[:, None, :], 0.0), axis=2)
    raw_exp = jnp.exp(picked)
    gate_weights = raw_exp / jnp.sum(raw_exp, axis=1, keepdims=True)
    share = jax.nn.sigmoid(
        jnp.dot(all_features, shared_gate_vector, preferred_element_type=jnp.float32)
    )
    hit_table = jnp.any(onehot, axis=1).astype(jnp.int32)
    running_count = jnp.cumsum(hit_table, axis=0)
    slot_rank = running_count - hit_table
    route_rank = jnp.sum(jnp.where(onehot, slot_rank[:, None, :], 0), axis=2)
    row_index = routes * capacity + route_rank

    request_ends = jnp.cumsum(lengths[0])
    request_count = lengths.shape[1]
    token_position = jnp.arange(token_count, dtype=jnp.int32)
    request_of = jnp.sum(
        (token_position[:, None] >= request_ends[None, :]).astype(jnp.int32), axis=1
    )
    request_match = request_of[:, None] == jnp.arange(request_count, dtype=jnp.int32)[None, :]
    adapter_of = jnp.sum(jnp.where(request_match, prompt_adapter_index[0][None, :], 0), axis=1)
    low_rank = lax.dot_general(
        all_features, full_in, (((1,), (1,)), ((), ())), preferred_element_type=jnp.float32
    )
    owner = jnp.arange(reduced_rank_value, dtype=jnp.int32) // rank_width
    adapter_mask = adapter_of[:, None] == owner[None, :]
    low_masked = jnp.where(adapter_mask, low_rank.astype(jnp.bfloat16), jnp.zeros((), jnp.bfloat16))
    picked_output_factor = jnp.take(adapter_output_factor, active_adapter_index, axis=0).reshape(
        reduced_rank_value, adapter_output_factor.shape[2]
    )
    adapter_update = jnp.dot(low_masked, picked_output_factor, preferred_element_type=jnp.float32)

    def shifted(x, shift):
        return lax.ppermute(x, "row", [(i, (i + shift) % row_count) for i in range(row_count)])

    def partner(x):
        return lax.ppermute(x, "row", [(i, i ^ 1) for i in range(row_count)])

    def row_blocks(x):
        group_half = x.shape[0] // 2
        from_below = shifted(x, 2)
        from_above = shifted(x, -2)
        far = jnp.concatenate(
            [shifted(from_below[:group_half], 2), shifted(from_above[group_half:], -2)], axis=0
        )
        same = [x, from_below, from_above, far]
        source = jnp.stack(
            [row_id, (row_id - 2) % row_count, (row_id + 2) % row_count, (row_id + 4) % row_count]
        ).astype(jnp.int32)
        return same + [partner(block) for block in same], jnp.concatenate([source, source ^ 1])

    slot_count = expert_count * capacity
    slot_id = jnp.arange(slot_count, dtype=jnp.int32)
    selection = jnp.any(row_index[None, :, :] == slot_id[:, None, None], axis=2).astype(jnp.bfloat16)
    chosen = jnp.dot(selection, tokens, preferred_element_type=jnp.float32).astype(jnp.bfloat16)
    outgoing = chosen.reshape(col_count, local_experts, capacity, local_width)
    own_block = lax.all_to_all(outgoing, "col", split_axis=0, concat_axis=0, tiled=True)
    slot_blocks, slot_source = row_blocks(own_block)
    arrival_groups = ((0, 4, 1, 2), (5, 6, 3, 7))

    def project(w):
        blocks = w.reshape(w.shape[0], row_count, local_width, w.shape[2])
        total = None
        for group in arrival_groups:
            features = jnp.concatenate([slot_blocks[j] for j in group], axis=3)
            order = jnp.stack([slot_source[j] for j in group])
            ordered = jnp.take(blocks, order, axis=1).reshape(w.shape[0], -1, w.shape[2])
            term = jnp.einsum("sexd,edf->sexf", features, ordered, preferred_element_type=jnp.float32)
            total = term if total is None else total + term
        return total

    gate_up = project(jnp.concatenate([routed_gate_weight, routed_up_weight], axis=2))
    gate_part = gate_up[..., : routed_gate_weight.shape[2]]
    up_part = gate_up[..., routed_gate_weight.shape[2] :]
    hidden = (jax.nn.silu(gate_part) * up_part).astype(jnp.bfloat16)
    local_hidden = hidden.shape[3]
    group_half = hidden.shape[0] // 2
    from_below = shifted(hidden, 2)
    from_above = shifted(hidden, -2)
    shared_gate_up = jnp.einsum(
        "tf,kfh->kth", all_features, shared_full[:2], preferred_element_type=jnp.float32
    )
    shared_gate_value, shared_up_value = shared_gate_up[0], shared_gate_up[1]
    shared_hidden_units = (
        jax.nn.silu(shared_gate_value) * (shared_up_value + ADAPTER_SCALE * adapter_update)
    ).astype(jnp.bfloat16)
    shared_part = lax.dot_general(
        shared_hidden_units,
        shared_full[2],
        (((1,), (1,)), ((), ())),
        preferred_element_type=jnp.float32,
    )
    shared_part = shared_part * share[:, None]
    far_low = shifted(from_below[:group_half], 2)
    far_high = shifted(from_above[group_half:], -2)
    shared_part, far_low, far_high = lax.optimization_barrier((shared_part, far_low, far_high))
    shared_sum = lax.psum_scatter(shared_part, "row", scatter_dimension=1, tiled=True)

    def down_slice(k):
        return lax.dynamic_slice_in_dim(
            routed_down_weight, ((row_id + k) % row_count) * local_width, local_width, axis=2
        )

    down_from = [down_slice(0)] + [shifted(down_slice(k), k) for k in range(1, row_count)]
    odd = row_id % 2 == 1

    def down_pick(k_even, k_odd):
        return jnp.where(odd, down_from[k_odd], down_from[k_even])

    def down_of(block, weight):
        return jnp.einsum("sexf,efd->sexd", block, weight, preferred_element_type=jnp.float32)

    whole_blocks = (
        (hidden, down_from[0], down_pick(7, 1)),
        (from_below, down_from[2], down_pick(1, 3)),
        (from_above, down_from[6], down_pick(5, 7)),
    )
    expert_value = None
    for block, weight, partner_weight in whole_blocks:
        term = down_of(block, weight) + down_of(partner(block), partner_weight)
        expert_value = term if expert_value is None else expert_value + term
    far_weight, far_partner_weight = down_from[4], down_pick(3, 5)
    low_part = down_of(far_low, far_weight) + down_of(partner(far_low), far_partner_weight)
    high_part = down_of(far_high, far_weight) + down_of(partner(far_high), far_partner_weight)
    expert_value = expert_value + jnp.concatenate([low_part, high_part], axis=0)
    returned = lax.all_to_all(
        expert_value.astype(jnp.bfloat16), "col", split_axis=0, concat_axis=0, tiled=True
    )
    flat_rows = returned.reshape(expert_count * capacity, local_width)
    routed = None
    for k in range(route_count):
        pick = (row_index[:, k][:, None] == slot_id[None, :]).astype(jnp.bfloat16)
        row = jnp.dot(pick, flat_rows, preferred_element_type=jnp.float32)
        term = gate_weights[:, k][:, None] * row
        routed = term if routed is None else routed + term

    return routed + shared_sum


def solution(mesh):
    return jax.shard_map(
        on_device,
        mesh=mesh,
        in_specs=(
            P("col", "row"),
            P(),
            P(),
            P("col", "row"),
            P("col", "row"),
            P("row", "col"),
            P("col", None, "row"),
            P("col", None, "row"),
            P("col", "row", None),
            P(None, None, "row"),
            P(None, None, "row"),
            P("col", None),
            P("col", None),
            P("col", None),
            P(),
        ),
        out_specs=P("col", "row"),
        check_vma=False,
    )
```
